256 devices in a mesh: dp: 64 (over x, z_lo, y, core), fsdp: 4 (over z_hi).
Axes of the slice: x: 4, y: 4, z: 8 (z_hi: 4, z_lo: 2; z = z_hi * 2 + z_lo), core: 2. Of those that a mesh axis runs over, the one named last changes fastest.
Arguments:
- bag_ids: int32 [32768, 64, 4], P(('dp', 'fsdp')), may hold values from 0 to 8191
- bag_counts: int32 [32768, 64], P(('dp', 'fsdp')), may hold values from 1 to 4
- emb_table: bfloat16 [8192, 8192], P(None, 'dp'), may hold values from -3 to 3
- cross_down: bfloat16 [8192, 512], P('fsdp'), may hold values from -0.0625 to 0.0625
- cross_up: bfloat16 [512, 8192], P(None, 'fsdp'), may hold values from -0.25 to 0.25
- cross_bias: float32 [8192], replicated, may hold values from -2 to 2
- cotangent: bfloat16 [32768, 8192], P(('dp', 'fsdp')), may hold values from -4 to 4
Outputs:
- table_grad: float32 [8192, 8192], P('fsdp', 'dp')
The draws below stay inside these ranges and needn't reach their ends.
Inputs may be any that keep to these rules, and one draw needn't show every extreme that they name: `bag_ids`: ids at positions at or past a bag's count are read by no step.
All inputs are finite; a program needn't handle non-finite values.
Results may differ from the reference program's by a relative error of at most 0.0045.
Values may be sent and summed in bfloat16 or wider, within the bound.
No kernel may reach another device: no remote copies, remote signals or barrier semaphores. Data moves between devices by JAX's collectives and lax.ppermute only.
A program may use at most 192 MiB of HBM per device.

```python
import math
import jax
import jax.numpy as jnp
import numpy as np
from jax import lax

EMB = 128
TABLES = 64
RANK = 512
HOT = 4
VOCAB = 8192
WIDTH = 8192
BATCH = 32768


def place_ends(drawn, stream_key, least, top_value):
    longest = drawn.shape.index(max(drawn.shape))
    spots = []
    for shift in (0, 1):
        where = [jax.random.randint(jax.random.fold_in(stream_key, axis), (), 0, length) for axis, length in enumerate(drawn.shape)]
        where[longest] = (where[longest] + shift) % drawn.shape[longest]
        spots.append(tuple(where))
    return drawn.at[spots[0]].set(least).at[spots[1]].set(top_value)


def levels(key, dims, split, smallest, high):
    loudness = 1.0
    for axis_at, parts in split:
        heights = jax.random.uniform(jax.random.fold_in(jax.random.fold_in(key, 6), axis_at), (parts,), jnp.float32, smallest / len(split), high / len(split))
        loudness = loudness * jnp.repeat(jnp.exp(heights), dims[axis_at] // parts).reshape((-1,) + (1,) * (len(dims) - 1 - axis_at))
    return loudness


def rank_table(amount, lean):
    loads = [(1 << 20) // math.isqrt(rank ** lean) + 1 for rank in range(1, amount + 1)]
    scale = 1 + sum(loads) // (1 << 30)
    return np.cumsum(np.array([max(1, weight // scale) for weight in loads]))


def skewed_ids(key, extent, number_of, skew):
    table = rank_table(number_of, skew)
    pick = jax.random.randint(jax.random.fold_in(key, 1), extent, 0, int(table[number_of - 1]))
    rank = jnp.searchsorted(jnp.asarray(table, jnp.int32), pick, side="right")
    return jax.random.permutation(jax.random.fold_in(key, 2), number_of)[rank].astype(jnp.int32)


def scatter_about(own_key, extent, spread, limit, shards=(), kind=jnp.bfloat16):
    array = spread * jax.random.normal(own_key, extent, jnp.float32)
    if shards:
        array = array * levels(own_key, extent, shards, -0.22, 0.18)
    return jnp.clip(array, -limit, limit).astype(kind)


def setup_inputs(seed: int = 0) -> dict:
    seeds = jax.random.split(jax.random.key(seed), 8)
    return {
        "bag_ids": place_ends(skewed_ids(seeds[0], (BATCH, TABLES, HOT), VOCAB, 2), jax.random.fold_in(seeds[0], 3), 0, VOCAB - 1).astype(jnp.int32),
        "bag_counts": place_ends(jax.random.randint(seeds[1], (BATCH, TABLES), 1, HOT + 1), jax.random.fold_in(seeds[1], 1), 1, HOT).astype(jnp.int32),
        "emb_table": scatter_about(seeds[2], (VOCAB, WIDTH), 0.5, 3.0, ((1, 64),)),
        "cross_down": scatter_about(seeds[3], (WIDTH, RANK), WIDTH ** -0.5, 0.0625, ((0, 4),)),
        "cross_up": scatter_about(seeds[4], (RANK, WIDTH), RANK ** -0.5, 0.25, ((1, 4),)),
        "cross_bias": scatter_about(seeds[5], (WIDTH,), 0.5, 2.0, (), jnp.float32),
        "cotangent": scatter_about(seeds[6], (BATCH, WIDTH), 0.5, 4.0, ((0, 256),)),
    }


def reference(bag_ids, bag_counts, emb_table, cross_down, cross_up, cross_bias, cotangent):
    batch = bag_ids.shape[0]
    width = TABLES * EMB

    def pool_table(table_idx):
        columns = lax.dynamic_slice_in_dim(emb_table, (table_idx * EMB).astype(jnp.int32), EMB, 1)
        running = jnp.zeros((batch, EMB), jnp.float32)
        for slot_idx in range(HOT):
            picked = jnp.take(columns, bag_ids[:, table_idx, slot_idx], axis=0).astype(jnp.float32)
            live_mask = bag_counts[:, table_idx] > slot_idx
            running = running + jnp.where(live_mask[:, None], picked, jnp.float32(0.0))
        return running.astype(jnp.bfloat16)

    pooled = lax.map(pool_table, jnp.arange(TABLES, dtype=jnp.int32))
    pooled = jnp.transpose(pooled, (1, 0, 2)).reshape(batch, width)

    block_rows = math.gcd(batch, 4096)
    block_count = batch // block_rows

    def dense_block(pair):
        inputs, upstream = pair
        low_rank = jnp.dot(inputs, cross_down, preferred_element_type=jnp.float32).astype(jnp.bfloat16)
        gate_value = jnp.dot(low_rank, cross_up, preferred_element_type=jnp.float32) + cross_bias
        upstream_f = upstream.astype(jnp.float32)
        grad_gate = (upstream_f * inputs.astype(jnp.float32)).astype(jnp.bfloat16)
        grad_low = jnp.dot(grad_gate, cross_up.T, preferred_element_type=jnp.float32).astype(jnp.bfloat16)
        back_term = jnp.dot(grad_low, cross_down.T, preferred_element_type=jnp.float32)
        return (upstream_f * (gate_value + 1.0) + back_term).astype(jnp.bfloat16)

    grad_pooled = lax.map(dense_block, (pooled.reshape(block_count, block_rows, width),
                                        cotangent.reshape(block_count, block_rows, width)))
    grad_pooled = grad_pooled.reshape(batch, width)

    def table_gradient(table_idx):
        grads = lax.dynamic_slice_in_dim(grad_pooled, (table_idx * EMB).astype(jnp.int32), EMB, 1).astype(jnp.float32)
        running = jnp.zeros((VOCAB, EMB), jnp.float32)
        for slot_idx in range(HOT):
            live_mask = bag_counts[:, table_idx] > slot_idx
            running = running.at[bag_ids[:, table_idx, slot_idx]].add(jnp.where(live_mask[:, None], grads, jnp.float32(0.0)))
        return running

    per_table = lax.map(table_gradient, jnp.arange(TABLES, dtype=jnp.int32))
    return jnp.transpose(per_table, (1, 0, 2)).reshape(VOCAB, width)
```

```python
import functools

import jax
import jax.numpy as jnp
from jax import lax
from jax.experimental import pallas as pl
from jax.experimental.pallas import tpu as pltpu
from jax.sharding import PartitionSpec as P

SCATTER_ACCS = 8
ZERO_ROWS = 8


def pool_kernel(ids_ref, tab_ref, out_ref, acc_ref, *, blk, slots):
    i = pl.program_id(0)

    def body(j, carry):
        s = i * blk + j
        r = tab_ref[pl.ds(ids_ref[s * slots], 1), :]
        for h in range(1, slots):
            r = r + tab_ref[pl.ds(ids_ref[s * slots + h], 1), :]
        acc_ref[pl.ds(j, 1), :] = r
        return carry

    lax.fori_loop(0, blk, body, 0, unroll=8)
    out_ref[...] = acc_ref[...].astype(out_ref.dtype)


def pool_rows(ids_flat, table_f32, slots, blk=512):
    count = ids_flat.shape[0] // slots
    width = table_f32.shape[1]
    return pl.pallas_call(
        functools.partial(pool_kernel, blk=blk, slots=slots),
        grid_spec=pltpu.PrefetchScalarGridSpec(
            num_scalar_prefetch=1,
            grid=(count // blk,),
            in_specs=[pl.BlockSpec(table_f32.shape, lambda i, ids: (0, 0))],
            out_specs=pl.BlockSpec((blk, width), lambda i, ids: (i, 0)),
            scratch_shapes=[pltpu.VMEM((blk, width), jnp.float32)],
        ),
        out_shape=jax.ShapeDtypeStruct((count, width), jnp.bfloat16),
    )(ids_flat, table_f32)


def scatter_kernel(ids_ref, g_ref, out_ref, *accs, slots):
    nacc = len(accs)
    count = g_ref.shape[0]
    rows = out_ref.shape[0]
    for a in accs:
        a[...] = jnp.zeros(a.shape, jnp.float32)

    def body(s2, carry):
        for k in range(2):
            s = s2 * 2 + k
            row = g_ref[pl.ds(s, 1), :]
            for h in range(slots):
                a = accs[(k * slots + h) % nacc]
                idx = ids_ref[s * slots + h]
                a[pl.ds(idx, 1), :] = a[pl.ds(idx, 1), :] + row
        return carry

    lax.fori_loop(0, count // 2, body, 0, unroll=4)
    total = accs[0][pl.ds(0, rows), :]
    for a in accs[1:]:
        total = total + a[pl.ds(0, rows), :]
    out_ref[...] = total


def scatter_rows(ids_flat, g_f32, rows, slots):
    count, width = g_f32.shape
    return pl.pallas_call(
        functools.partial(scatter_kernel, slots=slots),
        grid_spec=pltpu.PrefetchScalarGridSpec(
            num_scalar_prefetch=1,
            grid=(1,),
            in_specs=[pl.BlockSpec((count, width), lambda i, ids: (0, 0))],
            out_specs=pl.BlockSpec((rows, width), lambda i, ids: (0, 0)),
            scratch_shapes=[
                pltpu.VMEM((rows + ZERO_ROWS, width), jnp.float32)
                for _ in range(SCATTER_ACCS)
            ],
        ),
        out_shape=jax.ShapeDtypeStruct((rows, width), jnp.float32),
        compiler_params=pltpu.CompilerParams(vmem_limit_bytes=62 * 1024 * 1024),
    )(ids_flat, g_f32)


def on_device(bag_ids, bag_counts, emb_table, cross_down, cross_up, cross_bias, cotangent):
    row_count, table_count, slot_count = bag_ids.shape
    vocab_rows, col_piece = emb_table.shape
    dp_size = lax.axis_size("dp")
    rank = cross_down.shape[1]
    half = rank // 2

    dp_idx = lax.axis_index("dp")
    core = dp_idx % 2
    down_mine = lax.dynamic_slice_in_dim(cross_down, core * half, half, 1)
    up_mine = lax.dynamic_slice_in_dim(cross_up, core * half, half, 0)
    down_mine = lax.all_gather(down_mine, "fsdp", axis=0, tiled=True)
    up_mine = lax.all_gather(up_mine, "fsdp", axis=1, tiled=True)
    partner = [(i, i ^ 1) for i in range(dp_size)]
    down_other = lax.ppermute(down_mine, "dp", partner)
    up_other = lax.ppermute(up_mine, "dp", partner)

    slot_iota = lax.broadcasted_iota(jnp.int32, bag_ids.shape, 2)
    live_ids = jnp.where(slot_iota < bag_counts[:, :, None], bag_ids, vocab_rows)
    send_ids = live_ids.reshape(row_count, table_count * slot_count)
    got_ids = lax.all_to_all(send_ids, "dp", split_axis=1, concat_axis=0, tiled=True)
    sample_count = got_ids.shape[0]
    ids_flat = got_ids.reshape(-1)

    table_f32 = jnp.concatenate(
        [emb_table.astype(jnp.float32), jnp.zeros((ZERO_ROWS, col_piece), jnp.float32)]
    )
    pooled_local = pool_rows(ids_flat, table_f32, slot_count)
    pooled = lax.all_to_all(pooled_local, "dp", split_axis=0, concat_axis=1, tiled=True)

    upstream = cotangent.astype(jnp.float32)
    grad_gate = (upstream * pooled.astype(jnp.float32)).astype(jnp.bfloat16)
    low_mine = jnp.dot(pooled, down_mine, preferred_element_type=jnp.float32).astype(jnp.bfloat16)
    low_other = jnp.dot(pooled, down_other, preferred_element_type=jnp.float32).astype(jnp.bfloat16)
    gate_value = (
        jnp.dot(low_mine, up_mine, preferred_element_type=jnp.float32)
        + jnp.dot(low_other, up_other, preferred_element_type=jnp.float32)
        + cross_bias
    )
    contract = (((1,), (1,)), ((), ()))
    grad_low_mine = lax.dot_general(
        grad_gate, up_mine, contract, preferred_element_type=jnp.float32
    ).astype(jnp.bfloat16)
    grad_low_other = lax.dot_general(
        grad_gate, up_other, contract, preferred_element_type=jnp.float32
    ).astype(jnp.bfloat16)
    back_term = lax.dot_general(
        grad_low_mine, down_mine, contract, preferred_element_type=jnp.float32
    ) + lax.dot_general(grad_low_other, down_other, contract, preferred_element_type=jnp.float32)
    grad_pooled = (upstream * (gate_value + 1.0) + back_term).astype(jnp.bfloat16)
    grad_local = lax.all_to_all(grad_pooled, "dp", split_axis=1, concat_axis=0, tiled=True)
    partial_value = scatter_rows(
        ids_flat, grad_local.astype(jnp.float32), vocab_rows, slot_count
    )
    return lax.psum_scatter(partial_value, "fsdp", scatter_dimension=0, tiled=True)


def solution(mesh):
    placed = (
        P(("dp", "fsdp"), None, None),
        P(("dp", "fsdp"), None),
        P(None, "dp"),
        P("fsdp", None),
        P(None, "fsdp"),
        P(),
        P(("dp", "fsdp"), None),
    )
    return jax.shard_map(
        on_device, mesh=mesh, in_specs=placed, out_specs=P("fsdp", "dp"), check_vma=False
    )
```

```python
import functools

import jax
import jax.numpy as jnp
from jax import lax
from jax.experimental import pallas as pl
from jax.experimental.pallas import tpu as pltpu
from jax.sharding import PartitionSpec as P

SCATTER_ACCS = 8
ZERO_ROWS = 8


def pool_kernel(ids_ref, tab_ref, out_ref, acc_ref, *, blk, slots):
    i = pl.program_id(0)

    def body(j, carry):
        s = i * blk + j
        r = tab_ref[pl.ds(ids_ref[s * slots], 1), :]
        for h in range(1, slots):
            r = r + tab_ref[pl.ds(ids_ref[s * slots + h], 1), :]
        acc_ref[pl.ds(j, 1), :] = r
        return carry

    lax.fori_loop(0, blk, body, 0, unroll=8)
    out_ref[...] = acc_ref[...].astype(out_ref.dtype)


def pool_rows(ids_flat, table_f32, slots, blk=512):
    count = ids_flat.shape[0] // slots
    width = table_f32.shape[1]
    return pl.pallas_call(
        functools.partial(pool_kernel, blk=blk, slots=slots),
        grid_spec=pltpu.PrefetchScalarGridSpec(
            num_scalar_prefetch=1,
            grid=(count // blk,),
            in_specs=[pl.BlockSpec(table_f32.shape, lambda i, ids: (0, 0))],
            out_specs=pl.BlockSpec((blk, width), lambda i, ids: (i, 0)),
            scratch_shapes=[pltpu.VMEM((blk, width), jnp.float32)],
        ),
        out_shape=jax.ShapeDtypeStruct((count, width), jnp.bfloat16),
    )(ids_flat, table_f32)


def scatter_kernel(ids_ref, g_ref, out_ref, *accs, slots):
    nacc = len(accs)
    count = g_ref.shape[0]
    rows = out_ref.shape[0]
    for a in accs:
        a[...] = jnp.zeros(a.shape, jnp.float32)

    def body(s2, carry):
        for k in range(2):
            s = s2 * 2 + k
            row = g_ref[pl.ds(s, 1), :]
            for h in range(slots):
                a = accs[(k * slots + h) % nacc]
                idx = ids_ref[s * slots + h]
                a[pl.ds(idx, 1), :] = a[pl.ds(idx, 1), :] + row
        return carry

    lax.fori_loop(0, count // 2, body, 0, unroll=4)
    total = accs[0][pl.ds(0, rows), :]
    for a in accs[1:]:
        total = total + a[pl.ds(0, rows), :]
    out_ref[...] = total.astype(out_ref.dtype)


def scatter_rows(ids_flat, g_f32, rows, slots):
    count, width = g_f32.shape
    return pl.pallas_call(
        functools.partial(scatter_kernel, slots=slots),
        grid_spec=pltpu.PrefetchScalarGridSpec(
            num_scalar_prefetch=1,
            grid=(1,),
            in_specs=[pl.BlockSpec((count, width), lambda i, ids: (0, 0))],
            out_specs=pl.BlockSpec((rows, width), lambda i, ids: (0, 0)),
            scratch_shapes=[
                pltpu.VMEM((rows + ZERO_ROWS, width), jnp.float32)
                for _ in range(SCATTER_ACCS)
            ],
        ),
        out_shape=jax.ShapeDtypeStruct((rows, width), jnp.bfloat16),
        compiler_params=pltpu.CompilerParams(vmem_limit_bytes=62 * 1024 * 1024),
    )(ids_flat, g_f32)


def on_device(bag_ids, bag_counts, emb_table, cross_down, cross_up, cross_bias, cotangent):
    row_count, table_count, slot_count = bag_ids.shape
    vocab_rows, col_piece = emb_table.shape
    dp_size = lax.axis_size("dp")
    rank = cross_down.shape[1]
    half = rank // 2

    dp_idx = lax.axis_index("dp")
    core = dp_idx % 2
    down_mine = lax.dynamic_slice_in_dim(cross_down, core * half, half, 1)
    up_mine = lax.dynamic_slice_in_dim(cross_up, core * half, half, 0)
    down_mine = lax.all_gather(down_mine, "fsdp", axis=0, tiled=True)
    up_mine = lax.all_gather(up_mine, "fsdp", axis=1, tiled=True)
    partner = [(i, i ^ 1) for i in range(dp_size)]
    down_other = lax.ppermute(down_mine, "dp", partner)
    up_other = lax.ppermute(up_mine, "dp", partner)

    slot_iota = lax.broadcasted_iota(jnp.int32, bag_ids.shape, 2)
    live_ids = jnp.where(slot_iota < bag_counts[:, :, None], bag_ids, vocab_rows)
    send_ids = live_ids.reshape(row_count, table_count * slot_count)
    got_ids = lax.all_to_all(send_ids, "dp", split_axis=1, concat_axis=0, tiled=True)
    sample_count = got_ids.shape[0]
    ids_flat = got_ids.reshape(-1)

    table_f32 = jnp.concatenate(
        [emb_table.astype(jnp.float32), jnp.zeros((ZERO_ROWS, col_piece), jnp.float32)]
    )
    pooled_local = pool_rows(ids_flat, table_f32, slot_count)
    pooled = lax.all_to_all(pooled_local, "dp", split_axis=0, concat_axis=1, tiled=True)

    upstream = cotangent.astype(jnp.float32)
    grad_gate = (upstream * pooled.astype(jnp.float32)).astype(jnp.bfloat16)
    low_mine = jnp.dot(pooled, down_mine, preferred_element_type=jnp.float32).astype(jnp.bfloat16)
    low_other = jnp.dot(pooled, down_other, preferred_element_type=jnp.float32).astype(jnp.bfloat16)
    gate_value = (
        jnp.dot(low_mine, up_mine, preferred_element_type=jnp.float32)
        + jnp.dot(low_other, up_other, preferred_element_type=jnp.float32)
        + cross_bias
    )
    contract = (((1,), (1,)), ((), ()))
    grad_low_mine = lax.dot_general(
        grad_gate, up_mine, contract, preferred_element_type=jnp.float32
    ).astype(jnp.bfloat16)
    grad_low_other = lax.dot_general(
        grad_gate, up_other, contract, preferred_element_type=jnp.float32
    ).astype(jnp.bfloat16)
    back_term = lax.dot_general(
        grad_low_mine, down_mine, contract, preferred_element_type=jnp.float32
    ) + lax.dot_general(grad_low_other, down_other, contract, preferred_element_type=jnp.float32)
    grad_pooled = (upstream * (gate_value + 1.0) + back_term).astype(jnp.bfloat16)
    grad_local = lax.all_to_all(grad_pooled, "dp", split_axis=1, concat_axis=0, tiled=True)
    partial_value = scatter_rows(
        ids_flat, grad_local.astype(jnp.float32), vocab_rows, slot_count
    )
    summed = lax.psum_scatter(
        partial_value, "fsdp", scatter_dimension=0, tiled=True
    )
    return summed.astype(jnp.float32)


def solution(mesh):
    placed = (
        P(("dp", "fsdp"), None, None),
        P(("dp", "fsdp"), None),
        P(None, "dp"),
        P("fsdp", None),
        P(None, "fsdp"),
        P(),
        P(("dp", "fsdp"), None),
    )
    return jax.shard_map(
        on_device, mesh=mesh, in_specs=placed, out_specs=P("fsdp", "dp"), check_vma=False
    )
```

```python
import functools

import jax
import jax.numpy as jnp
from jax import lax
from jax.experimental import pallas as pl
from jax.experimental.pallas import tpu as pltpu
from jax.sharding import PartitionSpec as P

SCATTER_ACCS = 8
ZERO_ROWS = 8


def pool_kernel(ids_ref, tab_ref, out_ref, acc_ref, *, blk, slots):
    i = pl.program_id(0)

    def body(j, carry):
        s = i * blk + j
        r = tab_ref[pl.ds(ids_ref[s * slots], 1), :]
        for h in range(1, slots):
            r = r + tab_ref[pl.ds(ids_ref[s * slots + h], 1), :]
        acc_ref[pl.ds(j, 1), :] = r
        return carry

    lax.fori_loop(0, blk, body, 0, unroll=8)
    out_ref[...] = acc_ref[...].astype(out_ref.dtype)


def pool_rows(ids_flat, table_f32, slots, blk=512):
    count = ids_flat.shape[0] // slots
    width = table_f32.shape[1]
    return pl.pallas_call(
        functools.partial(pool_kernel, blk=blk, slots=slots),
        grid_spec=pltpu.PrefetchScalarGridSpec(
            num_scalar_prefetch=1,
            grid=(count // blk,),
            in_specs=[pl.BlockSpec(table_f32.shape, lambda i, ids: (0, 0))],
            out_specs=pl.BlockSpec((blk, width), lambda i, ids: (i, 0)),
            scratch_shapes=[pltpu.VMEM((blk, width), jnp.float32)],
        ),
        out_shape=jax.ShapeDtypeStruct((count, width), jnp.bfloat16),
    )(ids_flat, table_f32)


def scatter_kernel(ids_ref, g_ref, out_ref, *accs, slots):
    nacc = len(accs)
    count = g_ref.shape[0]
    rows = out_ref.shape[0]
    for a in accs:
        a[...] = jnp.zeros(a.shape, jnp.float32)

    def body(s2, carry):
        for k in range(2):
            s = s2 * 2 + k
            row = g_ref[pl.ds(s, 1), :]
            for h in range(slots):
                a = accs[(k * slots + h) % nacc]
                idx = ids_ref[s * slots + h]
                a[pl.ds(idx, 1), :] = a[pl.ds(idx, 1), :] + row
        return carry

    lax.fori_loop(0, count // 2, body, 0, unroll=4)
    total = accs[0][pl.ds(0, rows), :]
    for a in accs[1:]:
        total = total + a[pl.ds(0, rows), :]
    out_ref[...] = total.astype(out_ref.dtype)


def scatter_rows(ids_flat, g_f32, rows, slots):
    count, width = g_f32.shape
    return pl.pallas_call(
        functools.partial(scatter_kernel, slots=slots),
        grid_spec=pltpu.PrefetchScalarGridSpec(
            num_scalar_prefetch=1,
            grid=(1,),
            in_specs=[pl.BlockSpec((count, width), lambda i, ids: (0, 0))],
            out_specs=pl.BlockSpec((rows, width), lambda i, ids: (0, 0)),
            scratch_shapes=[
                pltpu.VMEM((rows + ZERO_ROWS, width), jnp.float32)
                for _ in range(SCATTER_ACCS)
            ],
        ),
        out_shape=jax.ShapeDtypeStruct((rows, width), jnp.bfloat16),
        compiler_params=pltpu.CompilerParams(vmem_limit_bytes=62 * 1024 * 1024),
    )(ids_flat, g_f32)


def on_device(bag_ids, bag_counts, emb_table, cross_down, cross_up, cross_bias, cotangent):
    row_count, table_count, slot_count = bag_ids.shape
    vocab_rows, col_piece = emb_table.shape
    dp_size = lax.axis_size("dp")
    rank = cross_down.shape[1]
    half = rank // 2

    dp_idx = lax.axis_index("dp")
    core = dp_idx % 2
    down_mine = lax.dynamic_slice_in_dim(cross_down, core * half, half, 1)
    up_mine = lax.dynamic_slice_in_dim(cross_up, core * half, half, 0)
    down_mine = lax.all_gather(down_mine, "fsdp", axis=0, tiled=True)
    up_mine = lax.all_gather(up_mine, "fsdp", axis=1, tiled=True)
    partner = [(i, i ^ 1) for i in range(dp_size)]
    down_other = lax.ppermute(down_mine, "dp", partner)
    up_other = lax.ppermute(up_mine, "dp", partner)

    slot_iota = lax.broadcasted_iota(jnp.int32, bag_ids.shape, 2)
    live_ids = jnp.where(slot_iota < bag_counts[:, :, None], bag_ids, vocab_rows)
    send_ids = live_ids.reshape(row_count, table_count * slot_count)
    got_ids = lax.all_to_all(send_ids, "dp", split_axis=1, concat_axis=0, tiled=True)
    sample_count = got_ids.shape[0]
    ids_flat = got_ids.reshape(-1)

    table_f32 = jnp.concatenate(
        [emb_table.astype(jnp.float32), jnp.zeros((ZERO_ROWS, col_piece), jnp.float32)]
    )
    pooled_local = pool_rows(ids_flat, table_f32, slot_count)
    pooled = lax.all_to_all(pooled_local, "dp", split_axis=0, concat_axis=1, tiled=True)

    upstream = cotangent.astype(jnp.float32)
    grad_gate = (upstream * pooled.astype(jnp.float32)).astype(jnp.bfloat16)
    low_mine = jnp.dot(pooled, down_mine, preferred_element_type=jnp.float32).astype(jnp.bfloat16)
    low_other = jnp.dot(pooled, down_other, preferred_element_type=jnp.float32).astype(jnp.bfloat16)
    low_mine, low_other = lax.optimization_barrier((low_mine, low_other))
    gate_value = (
        jnp.dot(low_mine, up_mine, preferred_element_type=jnp.float32)
        + jnp.dot(low_other, up_other, preferred_element_type=jnp.float32)
        + cross_bias
    )
    contract = (((1,), (1,)), ((), ()))
    grad_low_mine = lax.dot_general(
        grad_gate, up_mine, contract, preferred_element_type=jnp.float32
    ).astype(jnp.bfloat16)
    grad_low_other = lax.dot_general(
        grad_gate, up_other, contract, preferred_element_type=jnp.float32
    ).astype(jnp.bfloat16)
    grad_low_mine, grad_low_other = lax.optimization_barrier((grad_low_mine, grad_low_other))
    back_term = lax.dot_general(
        grad_low_mine, down_mine, contract, preferred_element_type=jnp.float32
    ) + lax.dot_general(grad_low_other, down_other, contract, preferred_element_type=jnp.float32)
    grad_pooled = (upstream * (gate_value + 1.0) + back_term).astype(jnp.bfloat16)
    grad_local = lax.all_to_all(grad_pooled, "dp", split_axis=1, concat_axis=0, tiled=True)
    partial_value = scatter_rows(
        ids_flat, grad_local.astype(jnp.float32), vocab_rows, slot_count
    )
    summed = lax.psum_scatter(
        partial_value, "fsdp", scatter_dimension=0, tiled=True
    )
    return summed.astype(jnp.float32)


def solution(mesh):
    placed = (
        P(("dp", "fsdp"), None, None),
        P(("dp", "fsdp"), None),
        P(None, "dp"),
        P("fsdp", None),
        P(None, "fsdp"),
        P(),
        P(("dp", "fsdp"), None),
    )
    return jax.shard_map(
        on_device, mesh=mesh, in_specs=placed, out_specs=P("fsdp", "dp"), check_vma=False
    )
```

```python
import functools

import jax
import jax.numpy as jnp
from jax import lax
from jax.experimental import pallas as pl
from jax.experimental.pallas import tpu as pltpu
from jax.sharding import PartitionSpec as P

SCATTER_ACCS = 8
ZERO_ROWS = 8


def pool_kernel(ids_ref, tab_ref, out_ref, acc_ref, *, blk, slots):
    i = pl.program_id(0)

    def body(j, carry):
        s = i * blk + j
        r = tab_ref[pl.ds(ids_ref[s * slots], 1), :]
        for h in range(1, slots):
            r = r + tab_ref[pl.ds(ids_ref[s * slots + h], 1), :]
        acc_ref[pl.ds(j, 1), :] = r
        return carry

    lax.fori_loop(0, blk, body, 0, unroll=8)
    out_ref[...] = acc_ref[...].astype(out_ref.dtype)


def pool_rows(ids_flat, table_f32, slots, blk=512):
    count = ids_flat.shape[0] // slots
    width = table_f32.shape[1]
    return pl.pallas_call(
        functools.partial(pool_kernel, blk=blk, slots=slots),
        grid_spec=pltpu.PrefetchScalarGridSpec(
            num_scalar_prefetch=1,
            grid=(count // blk,),
            in_specs=[pl.BlockSpec(table_f32.shape, lambda i, ids: (0, 0))],
            out_specs=pl.BlockSpec((blk, width), lambda i, ids: (i, 0)),
            scratch_shapes=[pltpu.VMEM((blk, width), jnp.float32)],
        ),
        out_shape=jax.ShapeDtypeStruct((count, width), jnp.bfloat16),
    )(ids_flat, table_f32)


def scatter_kernel(ids_ref, g_ref, *rest, slots, has_init):
    if has_init:
        init_ref, out_ref, *accs = rest
    else:
        out_ref, *accs = rest
    nacc = len(accs)
    count = g_ref.shape[0]
    rows = out_ref.shape[0]
    for a in accs:
        a[...] = jnp.zeros(a.shape, jnp.float32)
    if has_init:
        accs[0][pl.ds(0, rows), :] = init_ref[...]

    def body(s2, carry):
        for k in range(2):
            s = s2 * 2 + k
            row = g_ref[pl.ds(s, 1), :]
            for h in range(slots):
                a = accs[(k * slots + h) % nacc]
                idx = ids_ref[s * slots + h]
                a[pl.ds(idx, 1), :] = a[pl.ds(idx, 1), :] + row
        return carry

    lax.fori_loop(0, count // 2, body, 0, unroll=4)
    total = accs[0][pl.ds(0, rows), :]
    for a in accs[1:]:
        total = total + a[pl.ds(0, rows), :]
    out_ref[...] = total.astype(out_ref.dtype)


def scatter_rows(ids_flat, g_f32, rows, slots, init=None, out_dtype=jnp.bfloat16):
    count, width = g_f32.shape
    whole = lambda i, ids: (0, 0)
    in_specs = [pl.BlockSpec((count, width), whole)]
    operands = [ids_flat, g_f32]
    if init is not None:
        in_specs.append(pl.BlockSpec((rows, width), whole))
        operands.append(init)
    return pl.pallas_call(
        functools.partial(scatter_kernel, slots=slots, has_init=init is not None),
        grid_spec=pltpu.PrefetchScalarGridSpec(
            num_scalar_prefetch=1,
            grid=(1,),
            in_specs=in_specs,
            out_specs=pl.BlockSpec((rows, width), lambda i, ids: (0, 0)),
            scratch_shapes=[
                pltpu.VMEM((rows + ZERO_ROWS, width), jnp.float32)
                for _ in range(SCATTER_ACCS)
            ],
        ),
        out_shape=jax.ShapeDtypeStruct((rows, width), out_dtype),
        compiler_params=pltpu.CompilerParams(vmem_limit_bytes=62 * 1024 * 1024),
    )(*operands)


def on_device(bag_ids, bag_counts, emb_table, cross_down, cross_up, cross_bias, cotangent):
    row_count, table_count, slot_count = bag_ids.shape
    vocab_rows, col_piece = emb_table.shape
    dp_size = lax.axis_size("dp")
    rank = cross_down.shape[1]
    half = rank // 2

    dp_idx = lax.axis_index("dp")
    core = dp_idx % 2
    down_mine = lax.dynamic_slice_in_dim(cross_down, core * half, half, 1)
    up_mine = lax.dynamic_slice_in_dim(cross_up, core * half, half, 0)
    down_mine = lax.all_gather(down_mine, "fsdp", axis=0, tiled=True)
    up_mine = lax.all_gather(up_mine, "fsdp", axis=1, tiled=True)
    partner = [(i, i ^ 1) for i in range(dp_size)]
    down_other = lax.ppermute(down_mine, "dp", partner)
    up_other = lax.ppermute(up_mine, "dp", partner)

    slot_iota = lax.broadcasted_iota(jnp.int32, bag_ids.shape, 2)
    live_ids = jnp.where(slot_iota < bag_counts[:, :, None], bag_ids, vocab_rows)
    send_ids = live_ids.reshape(row_count, table_count * slot_count)
    got_ids = lax.all_to_all(send_ids, "dp", split_axis=1, concat_axis=0, tiled=True)
    sample_count = got_ids.shape[0]
    ids_flat = got_ids.reshape(-1)

    table_f32 = jnp.concatenate(
        [emb_table.astype(jnp.float32), jnp.zeros((ZERO_ROWS, col_piece), jnp.float32)]
    )
    pooled_local = pool_rows(ids_flat, table_f32, slot_count)
    pooled = lax.all_to_all(pooled_local, "dp", split_axis=0, concat_axis=1, tiled=True)

    def backward_rows(pooled_part, cot_part):
        upstream = cot_part.astype(jnp.float32)
        grad_gate = (upstream * pooled_part.astype(jnp.float32)).astype(jnp.bfloat16)
        low_mine = jnp.dot(pooled_part, down_mine, preferred_element_type=jnp.float32)
        low_other = jnp.dot(pooled_part, down_other, preferred_element_type=jnp.float32)
        low_mine, low_other = lax.optimization_barrier(
            (low_mine.astype(jnp.bfloat16), low_other.astype(jnp.bfloat16))
        )
        gate_value = (
            jnp.dot(low_mine, up_mine, preferred_element_type=jnp.float32)
            + jnp.dot(low_other, up_other, preferred_element_type=jnp.float32)
            + cross_bias
        )
        contract = (((1,), (1,)), ((), ()))
        grad_low_mine = lax.dot_general(
            grad_gate, up_mine, contract, preferred_element_type=jnp.float32
        ).astype(jnp.bfloat16)
        grad_low_other = lax.dot_general(
            grad_gate, up_other, contract, preferred_element_type=jnp.float32
        ).astype(jnp.bfloat16)
        grad_low_mine, grad_low_other = lax.optimization_barrier((grad_low_mine, grad_low_other))
        back_term = lax.dot_general(
            grad_low_mine, down_mine, contract, preferred_element_type=jnp.float32
        ) + lax.dot_general(grad_low_other, down_other, contract, preferred_element_type=jnp.float32)
        grad_pooled = (upstream * (gate_value + 1.0) + back_term).astype(jnp.bfloat16)
        return lax.all_to_all(grad_pooled, "dp", split_axis=1, concat_axis=0, tiled=True)

    split = row_count // 2
    ids_by_source = got_ids.reshape(dp_size, row_count, slot_count)
    partial_value = None
    for lo in (0, split):
        grad_local = backward_rows(pooled[lo:lo + split], cotangent[lo:lo + split])
        ids_part = ids_by_source[:, lo:lo + split].reshape(-1)
        last = lo == split
        partial_value = scatter_rows(
            ids_part, grad_local.astype(jnp.float32), vocab_rows, slot_count,
            init=partial_value, out_dtype=jnp.bfloat16 if last else jnp.float32,
        )
    summed = lax.psum_scatter(
        partial_value, "fsdp", scatter_dimension=0, tiled=True
    )
    return summed.astype(jnp.float32)


def solution(mesh):
    placed = (
        P(("dp", "fsdp"), None, None),
        P(("dp", "fsdp"), None),
        P(None, "dp"),
        P("fsdp", None),
        P(None, "fsdp"),
        P(),
        P(("dp", "fsdp"), None),
    )
    return jax.shard_map(
        on_device, mesh=mesh, in_specs=placed, out_specs=P("fsdp", "dp"), check_vma=False
    )
```

```python
import functools

import jax
import jax.numpy as jnp
from jax import lax
from jax.experimental import pallas as pl
from jax.experimental.pallas import tpu as pltpu
from jax.sharding import PartitionSpec as P

SCATTER_ACCS = 8
ZERO_ROWS = 8


def pool_kernel(ids_ref, tab_ref, out_ref, acc_ref, *, blk, slots):
    i = pl.program_id(0)

    def body(j, carry):
        s = i * blk + j
        r = tab_ref[pl.ds(ids_ref[s * slots], 1), :]
        for h in range(1, slots):
            r = r + tab_ref[pl.ds(ids_ref[s * slots + h], 1), :]
        acc_ref[pl.ds(j, 1), :] = r
        return carry

    lax.fori_loop(0, blk, body, 0, unroll=8)
    out_ref[...] = acc_ref[...].astype(out_ref.dtype)


def pool_rows(ids_flat, table_f32, slots, blk=512):
    count = ids_flat.shape[0] // slots
    width = table_f32.shape[1]
    return pl.pallas_call(
        functools.partial(pool_kernel, blk=blk, slots=slots),
        grid_spec=pltpu.PrefetchScalarGridSpec(
            num_scalar_prefetch=1,
            grid=(count // blk,),
            in_specs=[pl.BlockSpec(table_f32.shape, lambda i, ids: (0, 0))],
            out_specs=pl.BlockSpec((blk, width), lambda i, ids: (i, 0)),
            scratch_shapes=[pltpu.VMEM((blk, width), jnp.float32)],
        ),
        out_shape=jax.ShapeDtypeStruct((count, width), jnp.bfloat16),
    )(ids_flat, table_f32)


def scatter_kernel(ids_ref, g_ref, out_ref, *accs, slots):
    nacc = len(accs)
    count = g_ref.shape[0]
    rows = out_ref.shape[0]
    for a in accs:
        a[...] = jnp.zeros(a.shape, jnp.float32)

    def body(s2, carry):
        for k in range(2):
            s = s2 * 2 + k
            row = g_ref[pl.ds(s, 1), :]
            for h in range(slots):
                a = accs[(k * slots + h) % nacc]
                idx = ids_ref[s * slots + h]
                a[pl.ds(idx, 1), :] = a[pl.ds(idx, 1), :] + row
        return carry

    lax.fori_loop(0, count // 2, body, 0, unroll=4)
    total = accs[0][pl.ds(0, rows), :]
    for a in accs[1:]:
        total = total + a[pl.ds(0, rows), :]
    out_ref[...] = total.astype(out_ref.dtype)


def scatter_rows(ids_flat, g_f32, rows, slots):
    count, width = g_f32.shape
    return pl.pallas_call(
        functools.partial(scatter_kernel, slots=slots),
        grid_spec=pltpu.PrefetchScalarGridSpec(
            num_scalar_prefetch=1,
            grid=(1,),
            in_specs=[pl.BlockSpec((count, width), lambda i, ids: (0, 0))],
            out_specs=pl.BlockSpec((rows, width), lambda i, ids: (0, 0)),
            scratch_shapes=[
                pltpu.VMEM((rows + ZERO_ROWS, width), jnp.float32)
                for _ in range(SCATTER_ACCS)
            ],
        ),
        out_shape=jax.ShapeDtypeStruct((rows, width), jnp.bfloat16),
        compiler_params=pltpu.CompilerParams(vmem_limit_bytes=62 * 1024 * 1024),
    )(ids_flat, g_f32)


def on_device(bag_ids, bag_counts, emb_table, cross_down, cross_up, cross_bias, cotangent):
    row_count, table_count, slot_count = bag_ids.shape
    vocab_rows, col_piece = emb_table.shape
    dp_size = lax.axis_size("dp")
    rank = cross_down.shape[1]
    half = rank // 2

    fsdp_size = lax.axis_size("fsdp")
    dp_idx = lax.axis_index("dp")
    f_idx = lax.axis_index("fsdp")
    core = dp_idx % 2
    z_lo = (dp_idx // 8) % 2
    shard_rows = cross_down.shape[0]
    down_piece = lax.dynamic_slice_in_dim(cross_down, core * half, half, 1)
    up_piece = lax.dynamic_slice_in_dim(cross_up, core * half, half, 0)
    piece = jnp.concatenate([down_piece, up_piece.T], axis=1)

    def device_of(dp, f):
        return dp * fsdp_size + f

    def z_step(dp, f, step):
        lo = (dp // 8) % 2
        z = (2 * f + lo + step) % (2 * fsdp_size)
        return dp + (z % 2 - lo) * 8, z // 2

    ring_perm, pair_perm = [], []
    for dp in range(dp_size):
        for f in range(fsdp_size):
            lo = (dp // 8) % 2
            ring_perm.append((device_of(dp, f), device_of(*z_step(dp, f, 1 if lo else -1))))
            pair_perm.append((device_of(dp, f), device_of(dp ^ 8, f)))
    core_perm = [(device_of(dp, f), device_of(dp ^ 1, f))
                 for dp in range(dp_size) for f in range(fsdp_size)]
    both = ("dp", "fsdp")
    got_a = lax.ppermute(piece, both, ring_perm)
    got_b = lax.ppermute(got_a, both, pair_perm)
    got_c = lax.ppermute(got_b, both, ring_perm)
    step_a = jnp.where(z_lo == 0, -1, 1)
    shards = [
        (piece, f_idx),
        (got_a, (f_idx + step_a) % fsdp_size),
        (got_b, (f_idx - step_a) % fsdp_size),
        (got_c, (f_idx + 2) % fsdp_size),
    ]
    mine = jnp.zeros((shard_rows * fsdp_size, 2 * half), piece.dtype)
    other = jnp.zeros((shard_rows * fsdp_size, 2 * half), piece.dtype)
    for part, where in shards:
        mine = lax.dynamic_update_slice_in_dim(mine, part, where * shard_rows, 0)
        swapped = lax.ppermute(part, both, core_perm)
        other = lax.dynamic_update_slice_in_dim(other, swapped, where * shard_rows, 0)
    down_mine, up_t_mine = mine[:, :half], mine[:, half:]
    down_other, up_t_other = other[:, :half], other[:, half:]

    slot_iota = lax.broadcasted_iota(jnp.int32, bag_ids.shape, 2)
    live_ids = jnp.where(slot_iota < bag_counts[:, :, None], bag_ids, vocab_rows)
    send_ids = live_ids.reshape(row_count, table_count * slot_count)
    got_ids = lax.all_to_all(send_ids, "dp", split_axis=1, concat_axis=0, tiled=True)
    sample_count = got_ids.shape[0]
    ids_flat = got_ids.reshape(-1)

    table_f32 = jnp.concatenate(
        [emb_table.astype(jnp.float32), jnp.zeros((ZERO_ROWS, col_piece), jnp.float32)]
    )
    pooled_local = pool_rows(ids_flat, table_f32, slot_count)
    pooled = lax.all_to_all(pooled_local, "dp", split_axis=0, concat_axis=1, tiled=True)

    upstream = cotangent.astype(jnp.float32)
    grad_gate = (upstream * pooled.astype(jnp.float32)).astype(jnp.bfloat16)
    low_mine = jnp.dot(pooled, down_mine, preferred_element_type=jnp.float32).astype(jnp.bfloat16)
    low_other = jnp.dot(pooled, down_other, preferred_element_type=jnp.float32).astype(jnp.bfloat16)
    low_mine, low_other = lax.optimization_barrier((low_mine, low_other))
    contract = (((1,), (1,)), ((), ()))
    gate_value = (
        lax.dot_general(low_mine, up_t_mine, contract, preferred_element_type=jnp.float32)
        + lax.dot_general(low_other, up_t_other, contract, preferred_element_type=jnp.float32)
        + cross_bias
    )
    grad_low_mine = jnp.dot(grad_gate, up_t_mine, preferred_element_type=jnp.float32).astype(
        jnp.bfloat16
    )
    grad_low_other = jnp.dot(grad_gate, up_t_other, preferred_element_type=jnp.float32).astype(
        jnp.bfloat16
    )
    grad_low_mine, grad_low_other = lax.optimization_barrier((grad_low_mine, grad_low_other))
    back_term = lax.dot_general(
        grad_low_mine, down_mine, contract, preferred_element_type=jnp.float32
    ) + lax.dot_general(grad_low_other, down_other, contract, preferred_element_type=jnp.float32)
    grad_pooled = (upstream * (gate_value + 1.0) + back_term).astype(jnp.bfloat16)
    grad_local = lax.all_to_all(grad_pooled, "dp", split_axis=1, concat_axis=0, tiled=True)
    partial_value = scatter_rows(
        ids_flat, grad_local.astype(jnp.float32), vocab_rows, slot_count
    )
    summed = lax.psum_scatter(
        partial_value, "fsdp", scatter_dimension=0, tiled=True
    )
    return summed.astype(jnp.float32)


def solution(mesh):
    placed = (
        P(("dp", "fsdp"), None, None),
        P(("dp", "fsdp"), None),
        P(None, "dp"),
        P("fsdp", None),
        P(None, "fsdp"),
        P(),
        P(("dp", "fsdp"), None),
    )
    return jax.shard_map(
        on_device, mesh=mesh, in_specs=placed, out_specs=P("fsdp", "dp"), check_vma=False
    )
```

```python
import functools

import jax
import jax.numpy as jnp
from jax import lax
from jax.experimental import pallas as pl
from jax.experimental.pallas import tpu as pltpu
from jax.sharding import PartitionSpec as P

SCATTER_ACCS = 8
ZERO_ROWS = 8


def pool_kernel(ids_ref, tab_ref, out_ref, acc_ref, *, blk, slots):
    i = pl.program_id(0)

    def body(j, carry):
        s = i * blk + j
        r = tab_ref[pl.ds(ids_ref[s * slots], 1), :]
        for h in range(1, slots):
            r = r + tab_ref[pl.ds(ids_ref[s * slots + h], 1), :]
        acc_ref[pl.ds(j, 1), :] = r
        return carry

    lax.fori_loop(0, blk, body, 0, unroll=8)
    out_ref[...] = acc_ref[...].astype(out_ref.dtype)


def pool_rows(ids_flat, table_f32, slots, blk=512):
    count = ids_flat.shape[0] // slots
    width = table_f32.shape[1]
    return pl.pallas_call(
        functools.partial(pool_kernel, blk=blk, slots=slots),
        grid_spec=pltpu.PrefetchScalarGridSpec(
            num_scalar_prefetch=1,
            grid=(count // blk,),
            in_specs=[pl.BlockSpec(table_f32.shape, lambda i, ids: (0, 0))],
            out_specs=pl.BlockSpec((blk, width), lambda i, ids: (i, 0)),
            scratch_shapes=[pltpu.VMEM((blk, width), jnp.float32)],
        ),
        out_shape=jax.ShapeDtypeStruct((count, width), jnp.bfloat16),
    )(ids_flat, table_f32)


def scatter_kernel(ids_ref, g_ref, out_ref, *accs, slots):
    nacc = len(accs)
    count = g_ref.shape[0]
    rows = out_ref.shape[0]
    for a in accs:
        a[...] = jnp.zeros(a.shape, jnp.float32)

    def body(s2, carry):
        for k in range(2):
            s = s2 * 2 + k
            row = g_ref[pl.ds(s, 1), :]
            for h in range(slots):
                a = accs[(k * slots + h) % nacc]
                idx = ids_ref[s * slots + h]
                a[pl.ds(idx, 1), :] = a[pl.ds(idx, 1), :] + row
        return carry

    lax.fori_loop(0, count // 2, body, 0, unroll=4)
    total = accs[0][pl.ds(0, rows), :]
    for a in accs[1:]:
        total = total + a[pl.ds(0, rows), :]
    out_ref[...] = total.astype(out_ref.dtype)


def scatter_rows(ids_flat, g_f32, rows, slots):
    count, width = g_f32.shape
    return pl.pallas_call(
        functools.partial(scatter_kernel, slots=slots),
        grid_spec=pltpu.PrefetchScalarGridSpec(
            num_scalar_prefetch=1,
            grid=(1,),
            in_specs=[pl.BlockSpec((count, width), lambda i, ids: (0, 0))],
            out_specs=pl.BlockSpec((rows, width), lambda i, ids: (0, 0)),
            scratch_shapes=[
                pltpu.VMEM((rows + ZERO_ROWS, width), jnp.float32)
                for _ in range(SCATTER_ACCS)
            ],
        ),
        out_shape=jax.ShapeDtypeStruct((rows, width), jnp.bfloat16),
        compiler_params=pltpu.CompilerParams(vmem_limit_bytes=62 * 1024 * 1024),
    )(ids_flat, g_f32)


def on_device(bag_ids, bag_counts, emb_table, cross_down, cross_up, cross_bias, cotangent):
    row_count, table_count, slot_count = bag_ids.shape
    vocab_rows, col_piece = emb_table.shape
    dp_size = lax.axis_size("dp")
    rank = cross_down.shape[1]
    half = rank // 2

    dp_idx = lax.axis_index("dp")
    core = dp_idx % 2
    down_mine = lax.dynamic_slice_in_dim(cross_down, core * half, half, 1)
    up_t_mine = lax.dynamic_slice_in_dim(cross_up, core * half, half, 0).T
    down_mine = lax.all_gather(down_mine, "fsdp", axis=0, tiled=True)
    up_t_mine = lax.all_gather(up_t_mine, "fsdp", axis=0, tiled=True)
    partner = [(i, i ^ 1) for i in range(dp_size)]
    down_other = lax.ppermute(down_mine, "dp", partner)
    up_t_other = lax.ppermute(up_t_mine, "dp", partner)

    slot_iota = lax.broadcasted_iota(jnp.int32, bag_ids.shape, 2)
    live_ids = jnp.where(slot_iota < bag_counts[:, :, None], bag_ids, vocab_rows)
    send_ids = live_ids.reshape(row_count, table_count * slot_count)
    got_ids = lax.all_to_all(send_ids, "dp", split_axis=1, concat_axis=0, tiled=True)
    sample_count = got_ids.shape[0]
    ids_flat = got_ids.reshape(-1)

    table_f32 = jnp.concatenate(
        [emb_table.astype(jnp.float32), jnp.zeros((ZERO_ROWS, col_piece), jnp.float32)]
    )
    pooled_local = pool_rows(ids_flat, table_f32, slot_count)
    pooled = lax.all_to_all(pooled_local, "dp", split_axis=0, concat_axis=1, tiled=True)

    upstream = cotangent.astype(jnp.float32)
    grad_gate = (upstream * pooled.astype(jnp.float32)).astype(jnp.bfloat16)
    low_mine = jnp.dot(pooled, down_mine, preferred_element_type=jnp.float32).astype(jnp.bfloat16)
    low_other = jnp.dot(pooled, down_other, preferred_element_type=jnp.float32).astype(jnp.bfloat16)
    low_mine, low_other = lax.optimization_barrier((low_mine, low_other))
    contract = (((1,), (1,)), ((), ()))
    gate_value = (
        lax.dot_general(low_mine, up_t_mine, contract, preferred_element_type=jnp.float32)
        + lax.dot_general(low_other, up_t_other, contract, preferred_element_type=jnp.float32)
        + cross_bias
    )
    grad_low_mine = jnp.dot(grad_gate, up_t_mine, preferred_element_type=jnp.float32).astype(
        jnp.bfloat16
    )
    grad_low_other = jnp.dot(grad_gate, up_t_other, preferred_element_type=jnp.float32).astype(
        jnp.bfloat16
    )
    grad_low_mine, grad_low_other = lax.optimization_barrier((grad_low_mine, grad_low_other))
    back_term = lax.dot_general(
        grad_low_mine, down_mine, contract, preferred_element_type=jnp.float32
    ) + lax.dot_general(grad_low_other, down_other, contract, preferred_element_type=jnp.float32)
    grad_pooled = (upstream * (gate_value + 1.0) + back_term).astype(jnp.bfloat16)
    grad_local = lax.all_to_all(grad_pooled, "dp", split_axis=1, concat_axis=0, tiled=True)
    partial_value = scatter_rows(
        ids_flat, grad_local.astype(jnp.float32), vocab_rows, slot_count
    )
    summed = lax.psum_scatter(
        partial_value, "fsdp", scatter_dimension=0, tiled=True
    )
    return summed.astype(jnp.float32)


def solution(mesh):
    placed = (
        P(("dp", "fsdp"), None, None),
        P(("dp", "fsdp"), None),
        P(None, "dp"),
        P("fsdp", None),
        P(None, "fsdp"),
        P(),
        P(("dp", "fsdp"), None),
    )
    return jax.shard_map(
        on_device, mesh=mesh, in_specs=placed, out_specs=P("fsdp", "dp"), check_vma=False
    )
```

```python
import functools

import jax
import jax.numpy as jnp
from jax import lax
from jax.experimental import pallas as pl
from jax.experimental.pallas import tpu as pltpu
from jax.sharding import PartitionSpec as P

SCATTER_ACCS = 8
ZERO_ROWS = 8


def pool_kernel(ids_ref, tab_ref, out_ref, acc_ref, *, blk, slots):
    i = pl.program_id(0)

    def body(j, carry):
        s = i * blk + j
        r = tab_ref[pl.ds(ids_ref[s * slots], 1), :]
        for h in range(1, slots):
            r = r + tab_ref[pl.ds(ids_ref[s * slots + h], 1), :]
        acc_ref[pl.ds(j, 1), :] = r
        return carry

    lax.fori_loop(0, blk, body, 0, unroll=8)
    out_ref[...] = acc_ref[...].astype(out_ref.dtype)


def pool_rows(ids_flat, table_f32, slots, blk=512):
    count = ids_flat.shape[0] // slots
    width = table_f32.shape[1]
    return pl.pallas_call(
        functools.partial(pool_kernel, blk=blk, slots=slots),
        grid_spec=pltpu.PrefetchScalarGridSpec(
            num_scalar_prefetch=1,
            grid=(count // blk,),
            in_specs=[pl.BlockSpec(table_f32.shape, lambda i, ids: (0, 0))],
            out_specs=pl.BlockSpec((blk, width), lambda i, ids: (i, 0)),
            scratch_shapes=[pltpu.VMEM((blk, width), jnp.float32)],
        ),
        out_shape=jax.ShapeDtypeStruct((count, width), jnp.bfloat16),
    )(ids_flat, table_f32)


def scatter_kernel(ids_ref, g_ref, out_ref, *accs, slots):
    nacc = len(accs)
    count = g_ref.shape[0]
    rows = out_ref.shape[0]
    for a in accs:
        a[...] = jnp.zeros(a.shape, jnp.float32)

    def body(s2, carry):
        for k in range(2):
            s = s2 * 2 + k
            row = g_ref[pl.ds(s, 1), :]
            for h in range(slots):
                a = accs[(k * slots + h) % nacc]
                idx = ids_ref[s * slots + h]
                a[pl.ds(idx, 1), :] = a[pl.ds(idx, 1), :] + row
        return carry

    lax.fori_loop(0, count // 2, body, 0, unroll=4)
    total = accs[0][pl.ds(0, rows), :]
    for a in accs[1:]:
        total = total + a[pl.ds(0, rows), :]
    out_ref[...] = total.astype(out_ref.dtype)


def scatter_rows(ids_flat, g_f32, rows, slots):
    count, width = g_f32.shape
    return pl.pallas_call(
        functools.partial(scatter_kernel, slots=slots),
        grid_spec=pltpu.PrefetchScalarGridSpec(
            num_scalar_prefetch=1,
            grid=(1,),
            in_specs=[pl.BlockSpec((count, width), lambda i, ids: (0, 0))],
            out_specs=pl.BlockSpec((rows, width), lambda i, ids: (0, 0)),
            scratch_shapes=[
                pltpu.VMEM((rows + ZERO_ROWS, width), jnp.float32)
                for _ in range(SCATTER_ACCS)
            ],
        ),
        out_shape=jax.ShapeDtypeStruct((rows, width), jnp.bfloat16),
        compiler_params=pltpu.CompilerParams(vmem_limit_bytes=62 * 1024 * 1024),
    )(ids_flat, g_f32)


def on_device(bag_ids, bag_counts, emb_table, cross_down, cross_up, cross_bias, cotangent):
    row_count, table_count, slot_count = bag_ids.shape
    vocab_rows, col_piece = emb_table.shape
    dp_size = lax.axis_size("dp")
    rank = cross_down.shape[1]
    half = rank // 2

    dp_idx = lax.axis_index("dp")
    core = dp_idx % 2
    down_mine = lax.dynamic_slice_in_dim(cross_down, core * half, half, 1)
    up_mine = lax.dynamic_slice_in_dim(cross_up, core * half, half, 0)
    down_mine = lax.all_gather(down_mine, "fsdp", axis=0, tiled=True)
    up_mine = lax.all_gather(up_mine, "fsdp", axis=1, tiled=True)
    partner = [(i, i ^ 1) for i in range(dp_size)]
    down_other = lax.ppermute(down_mine, "dp", partner)
    up_other = lax.ppermute(up_mine, "dp", partner)

    slot_iota = lax.broadcasted_iota(jnp.int32, bag_ids.shape, 2)
    live_ids = jnp.where(slot_iota < bag_counts[:, :, None], bag_ids, vocab_rows)
    send_ids = live_ids.reshape(row_count, table_count * slot_count)
    got_ids = lax.all_to_all(send_ids, "dp", split_axis=1, concat_axis=0, tiled=True)
    sample_count = got_ids.shape[0]
    ids_flat = got_ids.reshape(-1)

    table_f32 = jnp.concatenate(
        [emb_table.astype(jnp.float32), jnp.zeros((ZERO_ROWS, col_piece), jnp.float32)]
    )
    pooled_local = pool_rows(ids_flat, table_f32, slot_count)
    pooled = lax.all_to_all(pooled_local, "dp", split_axis=0, concat_axis=1, tiled=True)

    upstream = cotangent.astype(jnp.float32)
    grad_gate = (upstream * pooled.astype(jnp.float32)).astype(jnp.bfloat16)
    low_mine = jnp.dot(pooled, down_mine, preferred_element_type=jnp.float32).astype(jnp.bfloat16)
    low_other = jnp.dot(pooled, down_other, preferred_element_type=jnp.float32).astype(jnp.bfloat16)
    low_mine, low_other = lax.optimization_barrier((low_mine, low_other))
    gate_value = (
        jnp.dot(low_mine, up_mine, preferred_element_type=jnp.float32)
        + jnp.dot(low_other, up_other, preferred_element_type=jnp.float32)
        + cross_bias
    )
    contract = (((1,), (1,)), ((), ()))
    grad_low_mine = lax.dot_general(
        grad_gate, up_mine, contract, preferred_element_type=jnp.float32
    ).astype(jnp.bfloat16)
    grad_low_other = lax.dot_general(
        grad_gate, up_other, contract, preferred_element_type=jnp.float32
    ).astype(jnp.bfloat16)
    grad_low_mine, grad_low_other = lax.optimization_barrier((grad_low_mine, grad_low_other))
    back_term = lax.dot_general(
        grad_low_mine, down_mine, contract, preferred_element_type=jnp.float32
    ) + lax.dot_general(grad_low_other, down_other, contract, preferred_element_type=jnp.float32)
    grad_pooled = (upstream * (gate_value + 1.0) + back_term).astype(jnp.bfloat16)
    grad_local = lax.all_to_all(grad_pooled, "dp", split_axis=1, concat_axis=0, tiled=True)
    partial_value = scatter_rows(
        ids_flat, grad_local.astype(jnp.float32), vocab_rows, slot_count
    )
    fsdp_size = lax.axis_size("fsdp")
    pieces = lax.all_to_all(
        partial_value.reshape(fsdp_size, vocab_rows // fsdp_size, col_piece),
        "fsdp", split_axis=0, concat_axis=0, tiled=True,
    )
    return jnp.sum(pieces.astype(jnp.float32), axis=0)


def solution(mesh):
    placed = (
        P(("dp", "fsdp"), None, None),
        P(("dp", "fsdp"), None),
        P(None, "dp"),
        P("fsdp", None),
        P(None, "fsdp"),
        P(),
        P(("dp", "fsdp"), None),
    )
    return jax.shard_map(
        on_device, mesh=mesh, in_specs=placed, out_specs=P("fsdp", "dp"), check_vma=False
    )
```

```python
import functools

import jax
import jax.numpy as jnp
from jax import lax
from jax.experimental import pallas as pl
from jax.experimental.pallas import tpu as pltpu
from jax.sharding import PartitionSpec as P

SCATTER_ACCS = 8
ZERO_ROWS = 8


def pool_kernel(ids_ref, tab_ref, out_ref, acc_ref, *, blk, slots):
    i = pl.program_id(0)

    def body(j, carry):
        s = i * blk + j
        r = tab_ref[pl.ds(ids_ref[s * slots], 1), :]
        for h in range(1, slots):
            r = r + tab_ref[pl.ds(ids_ref[s * slots + h], 1), :]
        acc_ref[pl.ds(j, 1), :] = r
        return carry

    lax.fori_loop(0, blk, body, 0, unroll=8)
    out_ref[...] = acc_ref[...].astype(out_ref.dtype)


def pool_rows(ids_flat, table_f32, slots, blk=512):
    count = ids_flat.shape[0] // slots
    width = table_f32.shape[1]
    return pl.pallas_call(
        functools.partial(pool_kernel, blk=blk, slots=slots),
        grid_spec=pltpu.PrefetchScalarGridSpec(
            num_scalar_prefetch=1,
            grid=(count // blk,),
            in_specs=[pl.BlockSpec(table_f32.shape, lambda i, ids: (0, 0))],
            out_specs=pl.BlockSpec((blk, width), lambda i, ids: (i, 0)),
            scratch_shapes=[pltpu.VMEM((blk, width), jnp.float32)],
        ),
        out_shape=jax.ShapeDtypeStruct((count, width), jnp.bfloat16),
    )(ids_flat, table_f32)


def scatter_kernel(ids_ref, g_ref, out_ref, *accs, slots):
    nacc = len(accs)
    count = g_ref.shape[0]
    rows = out_ref.shape[0]
    for a in accs:
        a[...] = jnp.zeros(a.shape, jnp.float32)

    tile_rows = 16

    def body(t, carry):
        tile = g_ref[pl.ds(pl.multiple_of(t * tile_rows, tile_rows), tile_rows), :]
        tile = tile.astype(jnp.float32)
        for k in range(tile_rows):
            s = t * tile_rows + k
            row = tile[k:k + 1, :]
            for h in range(slots):
                a = accs[((k % 2) * slots + h) % nacc]
                idx = ids_ref[s * slots + h]
                a[pl.ds(idx, 1), :] = a[pl.ds(idx, 1), :] + row
        return carry

    lax.fori_loop(0, count // tile_rows, body, 0)
    total = accs[0][pl.ds(0, rows), :]
    for a in accs[1:]:
        total = total + a[pl.ds(0, rows), :]
    out_ref[...] = total.astype(out_ref.dtype)


def scatter_rows(ids_flat, grads, rows, slots):
    count, width = grads.shape
    return pl.pallas_call(
        functools.partial(scatter_kernel, slots=slots),
        grid_spec=pltpu.PrefetchScalarGridSpec(
            num_scalar_prefetch=1,
            grid=(1,),
            in_specs=[pl.BlockSpec((count, width), lambda i, ids: (0, 0))],
            out_specs=pl.BlockSpec((rows, width), lambda i, ids: (0, 0)),
            scratch_shapes=[
                pltpu.VMEM((rows + ZERO_ROWS, width), jnp.float32)
                for _ in range(SCATTER_ACCS)
            ],
        ),
        out_shape=jax.ShapeDtypeStruct((rows, width), jnp.bfloat16),
        compiler_params=pltpu.CompilerParams(vmem_limit_bytes=62 * 1024 * 1024),
    )(ids_flat, grads)


def on_device(bag_ids, bag_counts, emb_table, cross_down, cross_up, cross_bias, cotangent):
    row_count, table_count, slot_count = bag_ids.shape
    vocab_rows, col_piece = emb_table.shape
    dp_size = lax.axis_size("dp")
    rank = cross_down.shape[1]
    half = rank // 2

    dp_idx = lax.axis_index("dp")
    core = dp_idx % 2
    down_mine = lax.dynamic_slice_in_dim(cross_down, core * half, half, 1)
    up_mine = lax.dynamic_slice_in_dim(cross_up, core * half, half, 0)
    down_mine = lax.all_gather(down_mine, "fsdp", axis=0, tiled=True)
    up_mine = lax.all_gather(up_mine, "fsdp", axis=1, tiled=True)
    partner = [(i, i ^ 1) for i in range(dp_size)]
    down_other = lax.ppermute(down_mine, "dp", partner)
    up_other = lax.ppermute(up_mine, "dp", partner)

    slot_iota = lax.broadcasted_iota(jnp.int32, bag_ids.shape, 2)
    live_ids = jnp.where(slot_iota < bag_counts[:, :, None], bag_ids, vocab_rows)
    send_ids = live_ids.reshape(row_count, table_count * slot_count)
    got_ids = lax.all_to_all(send_ids, "dp", split_axis=1, concat_axis=0, tiled=True)
    sample_count = got_ids.shape[0]
    ids_flat = got_ids.reshape(-1)

    table_f32 = jnp.concatenate(
        [emb_table.astype(jnp.float32), jnp.zeros((ZERO_ROWS, col_piece), jnp.float32)]
    )
    pooled_local = pool_rows(ids_flat, table_f32, slot_count)
    pooled = lax.all_to_all(pooled_local, "dp", split_axis=0, concat_axis=1, tiled=True)

    upstream = cotangent.astype(jnp.float32)
    grad_gate = (upstream * pooled.astype(jnp.float32)).astype(jnp.bfloat16)
    low_mine = jnp.dot(pooled, down_mine, preferred_element_type=jnp.float32).astype(jnp.bfloat16)
    low_other = jnp.dot(pooled, down_other, preferred_element_type=jnp.float32).astype(jnp.bfloat16)
    low_mine, low_other = lax.optimization_barrier((low_mine, low_other))
    gate_value = (
        jnp.dot(low_mine, up_mine, preferred_element_type=jnp.float32)
        + jnp.dot(low_other, up_other, preferred_element_type=jnp.float32)
        + cross_bias
    )
    contract = (((1,), (1,)), ((), ()))
    grad_low_mine = lax.dot_general(
        grad_gate, up_mine, contract, preferred_element_type=jnp.float32
    ).astype(jnp.bfloat16)
    grad_low_other = lax.dot_general(
        grad_gate, up_other, contract, preferred_element_type=jnp.float32
    ).astype(jnp.bfloat16)
    grad_low_mine, grad_low_other = lax.optimization_barrier((grad_low_mine, grad_low_other))
    back_term = lax.dot_general(
        grad_low_mine, down_mine, contract, preferred_element_type=jnp.float32
    ) + lax.dot_general(grad_low_other, down_other, contract, preferred_element_type=jnp.float32)
    grad_pooled = (upstream * (gate_value + 1.0) + back_term).astype(jnp.bfloat16)
    grad_local = lax.all_to_all(grad_pooled, "dp", split_axis=1, concat_axis=0, tiled=True)
    partial_value = scatter_rows(
        ids_flat, grad_local, vocab_rows, slot_count
    )
    summed = lax.psum_scatter(
        partial_value, "fsdp", scatter_dimension=0, tiled=True
    )
    return summed.astype(jnp.float32)


def solution(mesh):
    placed = (
        P(("dp", "fsdp"), None, None),
        P(("dp", "fsdp"), None),
        P(None, "dp"),
        P("fsdp", None),
        P(None, "fsdp"),
        P(),
        P(("dp", "fsdp"), None),
    )
    return jax.shard_map(
        on_device, mesh=mesh, in_specs=placed, out_specs=P("fsdp", "dp"), check_vma=False
    )
```

```python
import functools

import jax
import jax.numpy as jnp
from jax import lax
from jax.experimental import pallas as pl
from jax.experimental.pallas import tpu as pltpu
from jax.sharding import PartitionSpec as P

SCATTER_ACCS = 8
ZERO_ROWS = 8


def pool_kernel(ids_ref, tab_ref, out_ref, acc_ref, *, blk, slots):
    i = pl.program_id(0)

    def body(j, carry):
        s = i * blk + j
        r = tab_ref[pl.ds(ids_ref[s * slots], 1), :]
        for h in range(1, slots):
            r = r + tab_ref[pl.ds(ids_ref[s * slots + h], 1), :]
        acc_ref[pl.ds(j, 1), :] = r
        return carry

    lax.fori_loop(0, blk, body, 0, unroll=8)
    out_ref[...] = acc_ref[...].astype(out_ref.dtype)


def pool_rows(ids_flat, table_f32, slots, blk=512):
    count = ids_flat.shape[0] // slots
    width = table_f32.shape[1]
    return pl.pallas_call(
        functools.partial(pool_kernel, blk=blk, slots=slots),
        grid_spec=pltpu.PrefetchScalarGridSpec(
            num_scalar_prefetch=1,
            grid=(count // blk,),
            in_specs=[pl.BlockSpec(table_f32.shape, lambda i, ids: (0, 0))],
            out_specs=pl.BlockSpec((blk, width), lambda i, ids: (i, 0)),
            scratch_shapes=[pltpu.VMEM((blk, width), jnp.float32)],
        ),
        out_shape=jax.ShapeDtypeStruct((count, width), jnp.bfloat16),
    )(ids_flat, table_f32)


def scatter_kernel(ids_ref, g_ref, out_ref, *accs, slots):
    nacc = len(accs)
    count = g_ref.shape[0]
    rows = out_ref.shape[0]
    for a in accs:
        a[...] = jnp.zeros(a.shape, jnp.float32)

    tile_rows = 16

    def body(t, carry):
        tile = g_ref[pl.ds(pl.multiple_of(t * tile_rows, tile_rows), tile_rows), :]
        tile = tile.astype(jnp.float32)
        for k in range(tile_rows):
            s = t * tile_rows + k
            row = tile[k:k + 1, :]
            for h in range(slots):
                a = accs[((k % 2) * slots + h) % nacc]
                idx = ids_ref[s * slots + h]
                a[pl.ds(idx, 1), :] = a[pl.ds(idx, 1), :] + row
        return carry

    lax.fori_loop(0, count // tile_rows, body, 0)
    total = accs[0][pl.ds(0, rows), :]
    for a in accs[1:]:
        total = total + a[pl.ds(0, rows), :]
    out_ref[...] = total.astype(out_ref.dtype)


def scatter_rows(ids_flat, grads, rows, slots):
    count, width = grads.shape
    return pl.pallas_call(
        functools.partial(scatter_kernel, slots=slots),
        grid_spec=pltpu.PrefetchScalarGridSpec(
            num_scalar_prefetch=1,
            grid=(1,),
            in_specs=[pl.BlockSpec((count, width), lambda i, ids: (0, 0))],
            out_specs=pl.BlockSpec((rows, width), lambda i, ids: (0, 0)),
            scratch_shapes=[
                pltpu.VMEM((rows + ZERO_ROWS, width), jnp.float32)
                for _ in range(SCATTER_ACCS)
            ],
        ),
        out_shape=jax.ShapeDtypeStruct((rows, width), jnp.bfloat16),
        compiler_params=pltpu.CompilerParams(vmem_limit_bytes=62 * 1024 * 1024),
    )(ids_flat, grads)


def on_device(bag_ids, bag_counts, emb_table, cross_down, cross_up, cross_bias, cotangent):
    row_count, table_count, slot_count = bag_ids.shape
    vocab_rows, col_piece = emb_table.shape
    dp_size = lax.axis_size("dp")
    rank = cross_down.shape[1]
    half = rank // 2

    dp_idx = lax.axis_index("dp")
    core = dp_idx % 2
    down_mine = lax.dynamic_slice_in_dim(cross_down, core * half, half, 1)
    quarter = half // 2
    down_mine = lax.all_gather(down_mine, "fsdp", axis=0, tiled=True)
    partner = [(i, i ^ 1) for i in range(dp_size)]
    down_other = lax.ppermute(down_mine, "dp", partner)
    up_parts = []
    for q in range(2):
        piece = lax.dynamic_slice_in_dim(cross_up, core * half + q * quarter, quarter, 0)
        piece = lax.all_gather(piece, "fsdp", axis=1, tiled=True)
        up_parts.append((piece, lax.ppermute(piece, "dp", partner)))

    slot_iota = lax.broadcasted_iota(jnp.int32, bag_ids.shape, 2)
    live_ids = jnp.where(slot_iota < bag_counts[:, :, None], bag_ids, vocab_rows)
    send_ids = live_ids.reshape(row_count, table_count * slot_count)
    got_ids = lax.all_to_all(send_ids, "dp", split_axis=1, concat_axis=0, tiled=True)
    sample_count = got_ids.shape[0]
    ids_flat = got_ids.reshape(-1)

    table_f32 = jnp.concatenate(
        [emb_table.astype(jnp.float32), jnp.zeros((ZERO_ROWS, col_piece), jnp.float32)]
    )
    pooled_local = pool_rows(ids_flat, table_f32, slot_count)
    pooled = lax.all_to_all(pooled_local, "dp", split_axis=0, concat_axis=1, tiled=True)

    upstream = cotangent.astype(jnp.float32)
    grad_gate = (upstream * pooled.astype(jnp.float32)).astype(jnp.bfloat16)
    low_mine = jnp.dot(pooled, down_mine, preferred_element_type=jnp.float32).astype(jnp.bfloat16)
    low_other = jnp.dot(pooled, down_other, preferred_element_type=jnp.float32).astype(jnp.bfloat16)
    low_mine, low_other = lax.optimization_barrier((low_mine, low_other))
    contract = (((1,), (1,)), ((), ()))
    gate_value = cross_bias
    grad_low_mine, grad_low_other = [], []
    for q, (up_q_mine, up_q_other) in enumerate(up_parts):
        cols = slice(q * quarter, (q + 1) * quarter)
        gate_value = (
            gate_value
            + jnp.dot(low_mine[:, cols], up_q_mine, preferred_element_type=jnp.float32)
            + jnp.dot(low_other[:, cols], up_q_other, preferred_element_type=jnp.float32)
        )
        grad_low_mine.append(lax.dot_general(
            grad_gate, up_q_mine, contract, preferred_element_type=jnp.float32
        ).astype(jnp.bfloat16))
        grad_low_other.append(lax.dot_general(
            grad_gate, up_q_other, contract, preferred_element_type=jnp.float32
        ).astype(jnp.bfloat16))
    grad_low_mine = jnp.concatenate(grad_low_mine, axis=1)
    grad_low_other = jnp.concatenate(grad_low_other, axis=1)
    grad_low_mine, grad_low_other = lax.optimization_barrier((grad_low_mine, grad_low_other))
    back_term = lax.dot_general(
        grad_low_mine, down_mine, contract, preferred_element_type=jnp.float32
    ) + lax.dot_general(grad_low_other, down_other, contract, preferred_element_type=jnp.float32)
    grad_pooled = (upstream * (gate_value + 1.0) + back_term).astype(jnp.bfloat16)
    grad_local = lax.all_to_all(grad_pooled, "dp", split_axis=1, concat_axis=0, tiled=True)
    partial_value = scatter_rows(
        ids_flat, grad_local, vocab_rows, slot_count
    )
    summed = lax.psum_scatter(
        partial_value, "fsdp", scatter_dimension=0, tiled=True
    )
    return summed.astype(jnp.float32)


def solution(mesh):
    placed = (
        P(("dp", "fsdp"), None, None),
        P(("dp", "fsdp"), None),
        P(None, "dp"),
        P("fsdp", None),
        P(None, "fsdp"),
        P(),
        P(("dp", "fsdp"), None),
    )
    return jax.shard_map(
        on_device, mesh=mesh, in_specs=placed, out_specs=P("fsdp", "dp"), check_vma=False
    )
```

```python
import functools

import jax
import jax.numpy as jnp
from jax import lax
from jax.experimental import pallas as pl
from jax.experimental.pallas import tpu as pltpu
from jax.sharding import PartitionSpec as P

SCATTER_ACCS = 8
ZERO_ROWS = 8


def pool_kernel(ids_ref, tab_ref, out_ref, acc_ref, *, blk, slots):
    i = pl.program_id(0)

    def body(j, carry):
        s = i * blk + j
        r = tab_ref[pl.ds(ids_ref[s * slots], 1), :]
        for h in range(1, slots):
            r = r + tab_ref[pl.ds(ids_ref[s * slots + h], 1), :]
        acc_ref[pl.ds(j, 1), :] = r
        return carry

    lax.fori_loop(0, blk, body, 0, unroll=8)
    out_ref[...] = acc_ref[...].astype(out_ref.dtype)


def pool_rows(ids_flat, table_f32, slots, blk=512):
    count = ids_flat.shape[0] // slots
    width = table_f32.shape[1]
    return pl.pallas_call(
        functools.partial(pool_kernel, blk=blk, slots=slots),
        grid_spec=pltpu.PrefetchScalarGridSpec(
            num_scalar_prefetch=1,
            grid=(count // blk,),
            in_specs=[pl.BlockSpec(table_f32.shape, lambda i, ids: (0, 0))],
            out_specs=pl.BlockSpec((blk, width), lambda i, ids: (i, 0)),
            scratch_shapes=[pltpu.VMEM((blk, width), jnp.float32)],
        ),
        out_shape=jax.ShapeDtypeStruct((count, width), jnp.bfloat16),
    )(ids_flat, table_f32)


def scatter_kernel(ids_ref, g_ref, *rest, slots, per_source, run, offset, has_init):
    if has_init:
        init_ref, out_ref, *accs = rest
    else:
        out_ref, *accs = rest
    nacc = len(accs)
    count = g_ref.shape[0]
    rows = out_ref.shape[0]
    for a in accs:
        a[...] = jnp.zeros(a.shape, jnp.float32)
    if has_init:
        accs[0][pl.ds(0, rows), :] = init_ref[...]

    tile_rows = 16
    tiles_per_source = per_source // tile_rows

    def body(t, carry):
        tile = g_ref[pl.ds(pl.multiple_of(t * tile_rows, tile_rows), tile_rows), :]
        tile = tile.astype(jnp.float32)
        source = t // tiles_per_source
        first = source * run + offset + (t % tiles_per_source) * tile_rows
        for k in range(tile_rows):
            row = tile[k:k + 1, :]
            for h in range(slots):
                a = accs[((k % 2) * slots + h) % nacc]
                idx = ids_ref[(first + k) * slots + h]
                a[pl.ds(idx, 1), :] = a[pl.ds(idx, 1), :] + row
        return carry

    lax.fori_loop(0, count // tile_rows, body, 0)
    total = accs[0][pl.ds(0, rows), :]
    for a in accs[1:]:
        total = total + a[pl.ds(0, rows), :]
    out_ref[...] = total.astype(out_ref.dtype)


def scatter_rows(ids_flat, grads, rows, slots, per_source, run, offset, init=None):
    count, width = grads.shape
    whole = lambda i, ids: (0, 0)
    in_specs = [pl.BlockSpec((count, width), whole)]
    operands = [ids_flat, grads]
    if init is not None:
        in_specs.append(pl.BlockSpec((rows, width), whole))
        operands.append(init)
    out_dtype = jnp.float32 if init is None else jnp.bfloat16
    return pl.pallas_call(
        functools.partial(
            scatter_kernel, slots=slots, per_source=per_source, run=run, offset=offset,
            has_init=init is not None,
        ),
        grid_spec=pltpu.PrefetchScalarGridSpec(
            num_scalar_prefetch=1,
            grid=(1,),
            in_specs=in_specs,
            out_specs=pl.BlockSpec((rows, width), whole),
            scratch_shapes=[
                pltpu.VMEM((rows + ZERO_ROWS, width), jnp.float32)
                for _ in range(SCATTER_ACCS)
            ],
        ),
        out_shape=jax.ShapeDtypeStruct((rows, width), out_dtype),
        compiler_params=pltpu.CompilerParams(vmem_limit_bytes=62 * 1024 * 1024),
    )(*operands)


def on_device(bag_ids, bag_counts, emb_table, cross_down, cross_up, cross_bias, cotangent):
    row_count, table_count, slot_count = bag_ids.shape
    vocab_rows, col_piece = emb_table.shape
    dp_size = lax.axis_size("dp")
    rank = cross_down.shape[1]
    half = rank // 2

    dp_idx = lax.axis_index("dp")
    core = dp_idx % 2
    down_mine = lax.dynamic_slice_in_dim(cross_down, core * half, half, 1)
    up_mine = lax.dynamic_slice_in_dim(cross_up, core * half, half, 0)
    down_mine = lax.all_gather(down_mine, "fsdp", axis=0, tiled=True)
    up_mine = lax.all_gather(up_mine, "fsdp", axis=1, tiled=True)
    partner = [(i, i ^ 1) for i in range(dp_size)]
    down_other = lax.ppermute(down_mine, "dp", partner)
    up_other = lax.ppermute(up_mine, "dp", partner)

    slot_iota = lax.broadcasted_iota(jnp.int32, bag_ids.shape, 2)
    live_ids = jnp.where(slot_iota < bag_counts[:, :, None], bag_ids, vocab_rows)
    send_ids = live_ids.reshape(row_count, table_count * slot_count)
    got_ids = lax.all_to_all(send_ids, "dp", split_axis=1, concat_axis=0, tiled=True)
    sample_count = got_ids.shape[0]
    ids_flat = got_ids.reshape(-1)

    table_f32 = jnp.concatenate(
        [emb_table.astype(jnp.float32), jnp.zeros((ZERO_ROWS, col_piece), jnp.float32)]
    )
    pooled_local = pool_rows(ids_flat, table_f32, slot_count)
    pooled = lax.all_to_all(pooled_local, "dp", split_axis=0, concat_axis=1, tiled=True)

    upstream = cotangent.astype(jnp.float32)
    grad_gate = (upstream * pooled.astype(jnp.float32)).astype(jnp.bfloat16)
    low_mine = jnp.dot(pooled, down_mine, preferred_element_type=jnp.float32).astype(jnp.bfloat16)
    low_other = jnp.dot(pooled, down_other, preferred_element_type=jnp.float32).astype(jnp.bfloat16)
    low_mine, low_other = lax.optimization_barrier((low_mine, low_other))
    gate_value = (
        jnp.dot(low_mine, up_mine, preferred_element_type=jnp.float32)
        + jnp.dot(low_other, up_other, preferred_element_type=jnp.float32)
        + cross_bias
    )
    contract = (((1,), (1,)), ((), ()))
    grad_low_mine = lax.dot_general(
        grad_gate, up_mine, contract, preferred_element_type=jnp.float32
    ).astype(jnp.bfloat16)
    grad_low_other = lax.dot_general(
        grad_gate, up_other, contract, preferred_element_type=jnp.float32
    ).astype(jnp.bfloat16)
    grad_low_mine, grad_low_other = lax.optimization_barrier((grad_low_mine, grad_low_other))
    back_term = lax.dot_general(
        grad_low_mine, down_mine, contract, preferred_element_type=jnp.float32
    ) + lax.dot_general(grad_low_other, down_other, contract, preferred_element_type=jnp.float32)
    grad_pooled = (upstream * (gate_value + 1.0) + back_term).astype(jnp.bfloat16)
    split = row_count // 2
    first_half = lax.all_to_all(
        grad_pooled[:split], "dp", split_axis=1, concat_axis=0, tiled=True
    )
    second_half = lax.all_to_all(
        grad_pooled[split:], "dp", split_axis=1, concat_axis=0, tiled=True
    )
    partial_value = scatter_rows(
        ids_flat, first_half, vocab_rows, slot_count, split, row_count, 0
    )
    partial_value = scatter_rows(
        ids_flat, second_half, vocab_rows, slot_count, split, row_count, split,
        init=partial_value,
    )
    summed = lax.psum_scatter(
        partial_value, "fsdp", scatter_dimension=0, tiled=True
    )
    return summed.astype(jnp.float32)


def solution(mesh):
    placed = (
        P(("dp", "fsdp"), None, None),
        P(("dp", "fsdp"), None),
        P(None, "dp"),
        P("fsdp", None),
        P(None, "fsdp"),
        P(),
        P(("dp", "fsdp"), None),
    )
    return jax.shard_map(
        on_device, mesh=mesh, in_specs=placed, out_specs=P("fsdp", "dp"), check_vma=False
    )
```

```python
import functools

import jax
import jax.numpy as jnp
from jax import lax
from jax.experimental import pallas as pl
from jax.experimental.pallas import tpu as pltpu
from jax.sharding import PartitionSpec as P

SCATTER_ACCS = 8
ZERO_ROWS = 8


def pool_kernel(ids_ref, tab_ref, out_ref, acc_ref, *, blk, slots):
    i = pl.program_id(0)

    def body(j, carry):
        s = i * blk + j
        r = tab_ref[pl.ds(ids_ref[s * slots], 1), :]
        for h in range(1, slots):
            r = r + tab_ref[pl.ds(ids_ref[s * slots + h], 1), :]
        acc_ref[pl.ds(j, 1), :] = r
        return carry

    lax.fori_loop(0, blk, body, 0, unroll=8)
    out_ref[...] = acc_ref[...].astype(out_ref.dtype)


def pool_rows(ids_flat, table_f32, slots, blk=512):
    count = ids_flat.shape[0] // slots
    width = table_f32.shape[1]
    return pl.pallas_call(
        functools.partial(pool_kernel, blk=blk, slots=slots),
        grid_spec=pltpu.PrefetchScalarGridSpec(
            num_scalar_prefetch=1,
            grid=(count // blk,),
            in_specs=[pl.BlockSpec(table_f32.shape, lambda i, ids: (0, 0))],
            out_specs=pl.BlockSpec((blk, width), lambda i, ids: (i, 0)),
            scratch_shapes=[pltpu.VMEM((blk, width), jnp.float32)],
        ),
        out_shape=jax.ShapeDtypeStruct((count, width), jnp.bfloat16),
    )(ids_flat, table_f32)


def scatter_kernel(ids_ref, g_ref, out_ref, *accs, slots):
    nacc = len(accs)
    count = g_ref.shape[0]
    rows = out_ref.shape[0]
    for a in accs:
        a[...] = jnp.zeros(a.shape, jnp.float32)

    tile_rows = 16

    def body(t, carry):
        tile = g_ref[pl.ds(pl.multiple_of(t * tile_rows, tile_rows), tile_rows), :]
        tile = tile.astype(jnp.float32)
        for k in range(tile_rows):
            s = t * tile_rows + k
            row = tile[k:k + 1, :]
            for h in range(slots):
                a = accs[((k % 2) * slots + h) % nacc]
                idx = ids_ref[s * slots + h]
                a[pl.ds(idx, 1), :] = a[pl.ds(idx, 1), :] + row
        return carry

    lax.fori_loop(0, count // tile_rows, body, 0)
    total = accs[0][pl.ds(0, rows), :]
    for a in accs[1:]:
        total = total + a[pl.ds(0, rows), :]
    out_ref[...] = total.astype(out_ref.dtype)


def scatter_rows(ids_flat, grads, rows, slots):
    count, width = grads.shape
    return pl.pallas_call(
        functools.partial(scatter_kernel, slots=slots),
        grid_spec=pltpu.PrefetchScalarGridSpec(
            num_scalar_prefetch=1,
            grid=(1,),
            in_specs=[pl.BlockSpec((count, width), lambda i, ids: (0, 0))],
            out_specs=pl.BlockSpec((rows, width), lambda i, ids: (0, 0)),
            scratch_shapes=[
                pltpu.VMEM((rows + ZERO_ROWS, width), jnp.float32)
                for _ in range(SCATTER_ACCS)
            ],
        ),
        out_shape=jax.ShapeDtypeStruct((rows, width), jnp.bfloat16),
        compiler_params=pltpu.CompilerParams(vmem_limit_bytes=62 * 1024 * 1024),
    )(ids_flat, grads)


def on_device(bag_ids, bag_counts, emb_table, cross_down, cross_up, cross_bias, cotangent):
    row_count, table_count, slot_count = bag_ids.shape
    vocab_rows, col_piece = emb_table.shape
    dp_size = lax.axis_size("dp")
    rank = cross_down.shape[1]
    half = rank // 2

    dp_idx = lax.axis_index("dp")
    core = dp_idx % 2
    down_mine = lax.dynamic_slice_in_dim(cross_down, core * half, half, 1)
    up_mine = lax.dynamic_slice_in_dim(cross_up, core * half, half, 0)
    down_mine = lax.all_gather(down_mine, "fsdp", axis=0, tiled=True)
    up_mine = lax.all_gather(up_mine, "fsdp", axis=1, tiled=True)
    partner = [(i, i ^ 1) for i in range(dp_size)]
    down_other = lax.ppermute(down_mine, "dp", partner)
    up_other = lax.ppermute(up_mine, "dp", partner)

    slot_iota = lax.broadcasted_iota(jnp.int32, bag_ids.shape, 2)
    live_ids = jnp.where(slot_iota < bag_counts[:, :, None], bag_ids, vocab_rows)
    send_ids = live_ids.reshape(row_count, table_count * slot_count)
    got_ids = lax.all_to_all(send_ids, "dp", split_axis=1, concat_axis=0, tiled=True)
    sample_count = got_ids.shape[0]
    ids_flat = got_ids.reshape(-1)

    table_f32 = jnp.concatenate(
        [emb_table.astype(jnp.float32), jnp.zeros((ZERO_ROWS, col_piece), jnp.float32)]
    )
    pooled_local = pool_rows(ids_flat, table_f32, slot_count)
    pooled = lax.all_to_all(pooled_local, "dp", split_axis=0, concat_axis=1, tiled=True)

    upstream = cotangent.astype(jnp.float32)
    grad_gate = (upstream * pooled.astype(jnp.float32)).astype(jnp.bfloat16)
    low_mine = jnp.dot(pooled, down_mine, preferred_element_type=jnp.float32).astype(jnp.bfloat16)
    low_other = jnp.dot(pooled, down_other, preferred_element_type=jnp.float32).astype(jnp.bfloat16)
    low_mine = lax.optimization_barrier(low_mine)
    low_other = lax.optimization_barrier(low_other)
    gate_value = (
        jnp.dot(low_mine, up_mine, preferred_element_type=jnp.float32)
        + jnp.dot(low_other, up_other, preferred_element_type=jnp.float32)
        + cross_bias
    )
    contract = (((1,), (1,)), ((), ()))
    grad_low_mine = lax.dot_general(
        grad_gate, up_mine, contract, preferred_element_type=jnp.float32
    ).astype(jnp.bfloat16)
    grad_low_other = lax.dot_general(
        grad_gate, up_other, contract, preferred_element_type=jnp.float32
    ).astype(jnp.bfloat16)
    grad_low_mine = lax.optimization_barrier(grad_low_mine)
    grad_low_other = lax.optimization_barrier(grad_low_other)
    back_term = lax.dot_general(
        grad_low_mine, down_mine, contract, preferred_element_type=jnp.float32
    ) + lax.dot_general(grad_low_other, down_other, contract, preferred_element_type=jnp.float32)
    grad_pooled = (upstream * (gate_value + 1.0) + back_term).astype(jnp.bfloat16)
    grad_local = lax.all_to_all(grad_pooled, "dp", split_axis=1, concat_axis=0, tiled=True)
    partial_value = scatter_rows(
        ids_flat, grad_local, vocab_rows, slot_count
    )
    summed = lax.psum_scatter(
        partial_value, "fsdp", scatter_dimension=0, tiled=True
    )
    return summed.astype(jnp.float32)


def solution(mesh):
    placed = (
        P(("dp", "fsdp"), None, None),
        P(("dp", "fsdp"), None),
        P(None, "dp"),
        P("fsdp", None),
        P(None, "fsdp"),
        P(),
        P(("dp", "fsdp"), None),
    )
    return jax.shard_map(
        on_device, mesh=mesh, in_specs=placed, out_specs=P("fsdp", "dp"), check_vma=False
    )
```

```python
import functools

import jax
import jax.numpy as jnp
from jax import lax
from jax.experimental import pallas as pl
from jax.experimental.pallas import tpu as pltpu
from jax.sharding import PartitionSpec as P

SCATTER_ACCS = 8
ZERO_ROWS = 8


def pool_kernel(ids_ref, tab_ref, out_ref, acc_ref, *, blk, slots):
    i = pl.program_id(0)

    def body(j, carry):
        s = i * blk + j
        r = tab_ref[pl.ds(ids_ref[s * slots], 1), :]
        for h in range(1, slots):
            r = r + tab_ref[pl.ds(ids_ref[s * slots + h], 1), :]
        acc_ref[pl.ds(j, 1), :] = r
        return carry

    lax.fori_loop(0, blk, body, 0, unroll=8)
    out_ref[...] = acc_ref[...].astype(out_ref.dtype)


def pool_rows(ids_flat, table_f32, slots, blk=512):
    count = ids_flat.shape[0] // slots
    width = table_f32.shape[1]
    return pl.pallas_call(
        functools.partial(pool_kernel, blk=blk, slots=slots),
        grid_spec=pltpu.PrefetchScalarGridSpec(
            num_scalar_prefetch=1,
            grid=(count // blk,),
            in_specs=[pl.BlockSpec(table_f32.shape, lambda i, ids: (0, 0))],
            out_specs=pl.BlockSpec((blk, width), lambda i, ids: (i, 0)),
            scratch_shapes=[pltpu.VMEM((blk, width), jnp.float32)],
        ),
        out_shape=jax.ShapeDtypeStruct((count, width), jnp.bfloat16),
    )(ids_flat, table_f32)


def scatter_kernel(ids_ref, g_ref, out_ref, *accs, slots):
    nacc = len(accs)
    count = g_ref.shape[0]
    rows = out_ref.shape[0]
    for a in accs:
        a[...] = jnp.zeros(a.shape, jnp.float32)

    tile_rows = 16

    def body(t, carry):
        tile = g_ref[pl.ds(pl.multiple_of(t * tile_rows, tile_rows), tile_rows), :]
        tile = tile.astype(jnp.float32)
        for k in range(tile_rows):
            s = t * tile_rows + k
            row = tile[k:k + 1, :]
            for h in range(slots):
                a = accs[((k % 2) * slots + h) % nacc]
                idx = ids_ref[s * slots + h]
                a[pl.ds(idx, 1), :] = a[pl.ds(idx, 1), :] + row
        return carry

    lax.fori_loop(0, count // tile_rows, body, 0)
    total = accs[0][pl.ds(0, rows), :]
    for a in accs[1:]:
        total = total + a[pl.ds(0, rows), :]
    out_ref[...] = total.astype(out_ref.dtype)


def scatter_rows(ids_flat, grads, rows, slots):
    count, width = grads.shape
    return pl.pallas_call(
        functools.partial(scatter_kernel, slots=slots),
        grid_spec=pltpu.PrefetchScalarGridSpec(
            num_scalar_prefetch=1,
            grid=(1,),
            in_specs=[pl.BlockSpec((count, width), lambda i, ids: (0, 0))],
            out_specs=pl.BlockSpec((rows, width), lambda i, ids: (0, 0)),
            scratch_shapes=[
                pltpu.VMEM((rows + ZERO_ROWS, width), jnp.float32)
                for _ in range(SCATTER_ACCS)
            ],
        ),
        out_shape=jax.ShapeDtypeStruct((rows, width), jnp.bfloat16),
        compiler_params=pltpu.CompilerParams(vmem_limit_bytes=62 * 1024 * 1024),
    )(ids_flat, grads)


def on_device(bag_ids, bag_counts, emb_table, cross_down, cross_up, cross_bias, cotangent):
    row_count, table_count, slot_count = bag_ids.shape
    vocab_rows, col_piece = emb_table.shape
    dp_size = lax.axis_size("dp")
    rank = cross_down.shape[1]
    half = rank // 2

    dp_idx = lax.axis_index("dp")
    core = dp_idx % 2
    down_mine = lax.dynamic_slice_in_dim(cross_down, core * half, half, 1)
    up_mine = lax.dynamic_slice_in_dim(cross_up, core * half, half, 0)
    down_mine = lax.all_gather(down_mine, "fsdp", axis=0, tiled=True)
    up_mine = lax.all_gather(up_mine, "fsdp", axis=1, tiled=True)
    partner = [(i, i ^ 1) for i in range(dp_size)]

    def swap(x, axis, chunks=4):
        size = x.shape[axis] // chunks
        parts = [
            lax.ppermute(lax.slice_in_dim(x, c * size, (c + 1) * size, axis=axis), "dp", partner)
            for c in range(chunks)
        ]
        return jnp.concatenate(parts, axis=axis)

    down_other = swap(down_mine, 0)
    up_other = swap(up_mine, 1)

    slot_iota = lax.broadcasted_iota(jnp.int32, bag_ids.shape, 2)
    live_ids = jnp.where(slot_iota < bag_counts[:, :, None], bag_ids, vocab_rows)
    send_ids = live_ids.reshape(row_count, table_count * slot_count)
    got_ids = lax.all_to_all(send_ids, "dp", split_axis=1, concat_axis=0, tiled=True)
    sample_count = got_ids.shape[0]
    ids_flat = got_ids.reshape(-1)

    table_f32 = jnp.concatenate(
        [emb_table.astype(jnp.float32), jnp.zeros((ZERO_ROWS, col_piece), jnp.float32)]
    )
    pooled_local = pool_rows(ids_flat, table_f32, slot_count)
    pooled = lax.all_to_all(pooled_local, "dp", split_axis=0, concat_axis=1, tiled=True)

    upstream = cotangent.astype(jnp.float32)
    grad_gate = (upstream * pooled.astype(jnp.float32)).astype(jnp.bfloat16)
    low_mine = jnp.dot(pooled, down_mine, preferred_element_type=jnp.float32).astype(jnp.bfloat16)
    low_other = jnp.dot(pooled, down_other, preferred_element_type=jnp.float32).astype(jnp.bfloat16)
    low_mine = lax.optimization_barrier(low_mine)
    low_other = lax.optimization_barrier(low_other)
    gate_value = (
        jnp.dot(low_mine, up_mine, preferred_element_type=jnp.float32)
        + jnp.dot(low_other, up_other, preferred_element_type=jnp.float32)
        + cross_bias
    )
    contract = (((1,), (1,)), ((), ()))
    grad_low_mine = lax.dot_general(
        grad_gate, up_mine, contract, preferred_element_type=jnp.float32
    ).astype(jnp.bfloat16)
    grad_low_other = lax.dot_general(
        grad_gate, up_other, contract, preferred_element_type=jnp.float32
    ).astype(jnp.bfloat16)
    grad_low_mine = lax.optimization_barrier(grad_low_mine)
    grad_low_other = lax.optimization_barrier(grad_low_other)
    back_term = lax.dot_general(
        grad_low_mine, down_mine, contract, preferred_element_type=jnp.float32
    ) + lax.dot_general(grad_low_other, down_other, contract, preferred_element_type=jnp.float32)
    grad_pooled = (upstream * (gate_value + 1.0) + back_term).astype(jnp.bfloat16)
    grad_local = lax.all_to_all(grad_pooled, "dp", split_axis=1, concat_axis=0, tiled=True)
    partial_value = scatter_rows(
        ids_flat, grad_local, vocab_rows, slot_count
    )
    summed = lax.psum_scatter(
        partial_value, "fsdp", scatter_dimension=0, tiled=True
    )
    return summed.astype(jnp.float32)


def solution(mesh):
    placed = (
        P(("dp", "fsdp"), None, None),
        P(("dp", "fsdp"), None),
        P(None, "dp"),
        P("fsdp", None),
        P(None, "fsdp"),
        P(),
        P(("dp", "fsdp"), None),
    )
    return jax.shard_map(
        on_device, mesh=mesh, in_specs=placed, out_specs=P("fsdp", "dp"), check_vma=False
    )
```

```python
import functools

import jax
import jax.numpy as jnp
from jax import lax
from jax.experimental import pallas as pl
from jax.experimental.pallas import tpu as pltpu
from jax.sharding import PartitionSpec as P

SCATTER_ACCS = 8
ZERO_ROWS = 8


def pool_kernel(ids_ref, tab_ref, out_ref, acc_ref, *, blk, slots):
    i = pl.program_id(0)

    def body(j, carry):
        s = i * blk + j
        r = tab_ref[pl.ds(ids_ref[s * slots], 1), :]
        for h in range(1, slots):
            r = r + tab_ref[pl.ds(ids_ref[s * slots + h], 1), :]
        acc_ref[pl.ds(j, 1), :] = r
        return carry

    lax.fori_loop(0, blk, body, 0, unroll=8)
    out_ref[...] = acc_ref[...].astype(out_ref.dtype)


def pool_rows(ids_flat, table_f32, slots, blk=512):
    count = ids_flat.shape[0] // slots
    width = table_f32.shape[1]
    return pl.pallas_call(
        functools.partial(pool_kernel, blk=blk, slots=slots),
        grid_spec=pltpu.PrefetchScalarGridSpec(
            num_scalar_prefetch=1,
            grid=(count // blk,),
            in_specs=[pl.BlockSpec(table_f32.shape, lambda i, ids: (0, 0))],
            out_specs=pl.BlockSpec((blk, width), lambda i, ids: (i, 0)),
            scratch_shapes=[pltpu.VMEM((blk, width), jnp.float32)],
        ),
        out_shape=jax.ShapeDtypeStruct((count, width), jnp.bfloat16),
    )(ids_flat, table_f32)


def scatter_kernel(ids_ref, g_ref, out_ref, *accs, slots):
    nacc = len(accs)
    count = g_ref.shape[0]
    rows = out_ref.shape[0]
    for a in accs:
        a[...] = jnp.zeros(a.shape, jnp.float32)

    tile_rows = 16

    def body(t, carry):
        tile = g_ref[pl.ds(pl.multiple_of(t * tile_rows, tile_rows), tile_rows), :]
        tile = tile.astype(jnp.float32)
        for k in range(tile_rows):
            s = t * tile_rows + k
            row = tile[k:k + 1, :]
            for h in range(slots):
                a = accs[((k % 2) * slots + h) % nacc]
                idx = ids_ref[s * slots + h]
                a[pl.ds(idx, 1), :] = a[pl.ds(idx, 1), :] + row
        return carry

    lax.fori_loop(0, count // tile_rows, body, 0)
    total = accs[0][pl.ds(0, rows), :]
    for a in accs[1:]:
        total = total + a[pl.ds(0, rows), :]
    out_ref[...] = total.astype(out_ref.dtype)


def scatter_rows(ids_flat, grads, rows, slots):
    count, width = grads.shape
    return pl.pallas_call(
        functools.partial(scatter_kernel, slots=slots),
        grid_spec=pltpu.PrefetchScalarGridSpec(
            num_scalar_prefetch=1,
            grid=(1,),
            in_specs=[pl.BlockSpec((count, width), lambda i, ids: (0, 0))],
            out_specs=pl.BlockSpec((rows, width), lambda i, ids: (0, 0)),
            scratch_shapes=[
                pltpu.VMEM((rows + ZERO_ROWS, width), jnp.float32)
                for _ in range(SCATTER_ACCS)
            ],
        ),
        out_shape=jax.ShapeDtypeStruct((rows, width), jnp.bfloat16),
        compiler_params=pltpu.CompilerParams(vmem_limit_bytes=62 * 1024 * 1024),
    )(ids_flat, grads)


def on_device(bag_ids, bag_counts, emb_table, cross_down, cross_up, cross_bias, cotangent):
    row_count, table_count, slot_count = bag_ids.shape
    vocab_rows, col_piece = emb_table.shape
    dp_size = lax.axis_size("dp")
    rank = cross_down.shape[1]
    half = rank // 2

    dp_idx = lax.axis_index("dp")
    core = dp_idx % 2
    quarter = half // 2
    down_piece = lax.dynamic_slice_in_dim(cross_down, core * half, half, 1)
    up_piece = lax.dynamic_slice_in_dim(cross_up, core * half, half, 0)
    first = jnp.concatenate([up_piece.T, down_piece[:, :quarter]], axis=1)
    first = lax.all_gather(first, "fsdp", axis=0, tiled=True)
    second = lax.all_gather(down_piece[:, quarter:], "fsdp", axis=0, tiled=True)
    partner = [(i, i ^ 1) for i in range(dp_size)]
    first_other = lax.ppermute(first, "dp", partner)
    second_other = lax.ppermute(second, "dp", partner)
    up_t_mine, up_t_other = first[:, :half], first_other[:, :half]
    down_mine = (first[:, half:], second)
    down_other = (first_other[:, half:], second_other)

    slot_iota = lax.broadcasted_iota(jnp.int32, bag_ids.shape, 2)
    live_ids = jnp.where(slot_iota < bag_counts[:, :, None], bag_ids, vocab_rows)
    send_ids = live_ids.reshape(row_count, table_count * slot_count)
    got_ids = lax.all_to_all(send_ids, "dp", split_axis=1, concat_axis=0, tiled=True)
    sample_count = got_ids.shape[0]
    ids_flat = got_ids.reshape(-1)

    table_f32 = jnp.concatenate(
        [emb_table.astype(jnp.float32), jnp.zeros((ZERO_ROWS, col_piece), jnp.float32)]
    )
    pooled_local = pool_rows(ids_flat, table_f32, slot_count)
    pooled = lax.all_to_all(pooled_local, "dp", split_axis=0, concat_axis=1, tiled=True)

    upstream = cotangent.astype(jnp.float32)
    grad_gate = (upstream * pooled.astype(jnp.float32)).astype(jnp.bfloat16)
    def low_of(downs):
        return jnp.concatenate(
            [jnp.dot(pooled, d, preferred_element_type=jnp.float32) for d in downs], axis=1
        ).astype(jnp.bfloat16)

    low_mine = low_of(down_mine)
    low_other = low_of(down_other)
    low_mine = lax.optimization_barrier(low_mine)
    low_other = lax.optimization_barrier(low_other)
    contract = (((1,), (1,)), ((), ()))
    gate_value = (
        lax.dot_general(low_mine, up_t_mine, contract, preferred_element_type=jnp.float32)
        + lax.dot_general(low_other, up_t_other, contract, preferred_element_type=jnp.float32)
        + cross_bias
    )
    grad_low_mine = jnp.dot(grad_gate, up_t_mine, preferred_element_type=jnp.float32).astype(
        jnp.bfloat16
    )
    grad_low_other = jnp.dot(grad_gate, up_t_other, preferred_element_type=jnp.float32).astype(
        jnp.bfloat16
    )
    grad_low_mine = lax.optimization_barrier(grad_low_mine)
    grad_low_other = lax.optimization_barrier(grad_low_other)
    back_term = None
    for grad_low, downs in ((grad_low_mine, down_mine), (grad_low_other, down_other)):
        for q, d in enumerate(downs):
            part = lax.dot_general(
                grad_low[:, q * quarter:(q + 1) * quarter], d, contract,
                preferred_element_type=jnp.float32,
            )
            back_term = part if back_term is None else back_term + part
    grad_pooled = (upstream * (gate_value + 1.0) + back_term).astype(jnp.bfloat16)
    grad_local = lax.all_to_all(grad_pooled, "dp", split_axis=1, concat_axis=0, tiled=True)
    partial_value = scatter_rows(
        ids_flat, grad_local, vocab_rows, slot_count
    )
    summed = lax.psum_scatter(
        partial_value, "fsdp", scatter_dimension=0, tiled=True
    )
    return summed.astype(jnp.float32)


def solution(mesh):
    placed = (
        P(("dp", "fsdp"), None, None),
        P(("dp", "fsdp"), None),
        P(None, "dp"),
        P("fsdp", None),
        P(None, "fsdp"),
        P(),
        P(("dp", "fsdp"), None),
    )
    return jax.shard_map(
        on_device, mesh=mesh, in_specs=placed, out_specs=P("fsdp", "dp"), check_vma=False
    )
```

```python
import functools

import jax
import jax.numpy as jnp
from jax import lax
from jax.experimental import pallas as pl
from jax.experimental.pallas import tpu as pltpu
from jax.sharding import PartitionSpec as P

SCATTER_ACCS = 8
ZERO_ROWS = 8


def pool_kernel(ids_ref, tab_ref, out_ref, acc_ref, *, blk, slots):
    i = pl.program_id(0)

    def body(j, carry):
        s = i * blk + j
        r = tab_ref[pl.ds(ids_ref[s * slots], 1), :]
        for h in range(1, slots):
            r = r + tab_ref[pl.ds(ids_ref[s * slots + h], 1), :]
        acc_ref[pl.ds(j, 1), :] = r
        return carry

    lax.fori_loop(0, blk, body, 0, unroll=8)
    out_ref[...] = acc_ref[...].astype(out_ref.dtype)


def pool_rows(ids_flat, table_f32, slots, blk=512):
    count = ids_flat.shape[0] // slots
    width = table_f32.shape[1]
    return pl.pallas_call(
        functools.partial(pool_kernel, blk=blk, slots=slots),
        grid_spec=pltpu.PrefetchScalarGridSpec(
            num_scalar_prefetch=1,
            grid=(count // blk,),
            in_specs=[pl.BlockSpec(table_f32.shape, lambda i, ids: (0, 0))],
            out_specs=pl.BlockSpec((blk, width), lambda i, ids: (i, 0)),
            scratch_shapes=[pltpu.VMEM((blk, width), jnp.float32)],
        ),
        out_shape=jax.ShapeDtypeStruct((count, width), jnp.bfloat16),
    )(ids_flat, table_f32)


def scatter_kernel(ids_ref, g_ref, out_ref, *accs, slots):
    nacc = len(accs)
    count = g_ref.shape[0]
    rows = out_ref.shape[0]
    for a in accs:
        a[...] = jnp.zeros(a.shape, jnp.float32)

    tile_rows = 16

    def body(t, carry):
        tile = g_ref[pl.ds(pl.multiple_of(t * tile_rows, tile_rows), tile_rows), :]
        tile = tile.astype(jnp.float32)
        for k in range(tile_rows):
            s = t * tile_rows + k
            row = tile[k:k + 1, :]
            for h in range(slots):
                a = accs[((k % 2) * slots + h) % nacc]
                idx = ids_ref[s * slots + h]
                a[pl.ds(idx, 1), :] = a[pl.ds(idx, 1), :] + row
        return carry

    lax.fori_loop(0, count // tile_rows, body, 0)
    total = accs[0][pl.ds(0, rows), :]
    for a in accs[1:]:
        total = total + a[pl.ds(0, rows), :]
    out_ref[...] = total.astype(out_ref.dtype)


def scatter_rows(ids_flat, grads, rows, slots):
    count, width = grads.shape
    return pl.pallas_call(
        functools.partial(scatter_kernel, slots=slots),
        grid_spec=pltpu.PrefetchScalarGridSpec(
            num_scalar_prefetch=1,
            grid=(1,),
            in_specs=[pl.BlockSpec((count, width), lambda i, ids: (0, 0))],
            out_specs=pl.BlockSpec((rows, width), lambda i, ids: (0, 0)),
            scratch_shapes=[
                pltpu.VMEM((rows + ZERO_ROWS, width), jnp.float32)
                for _ in range(SCATTER_ACCS)
            ],
        ),
        out_shape=jax.ShapeDtypeStruct((rows, width), jnp.bfloat16),
        compiler_params=pltpu.CompilerParams(vmem_limit_bytes=62 * 1024 * 1024),
    )(ids_flat, grads)


def on_device(bag_ids, bag_counts, emb_table, cross_down, cross_up, cross_bias, cotangent):
    row_count, table_count, slot_count = bag_ids.shape
    vocab_rows, col_piece = emb_table.shape
    dp_size = lax.axis_size("dp")
    rank = cross_down.shape[1]
    half = rank // 2

    dp_idx = lax.axis_index("dp")
    core = dp_idx % 2
    down_mine = lax.dynamic_slice_in_dim(cross_down, core * half, half, 1)
    up_mine = lax.dynamic_slice_in_dim(cross_up, core * half, half, 0)
    down_mine = lax.all_gather(down_mine, "fsdp", axis=0, tiled=True)
    up_mine = lax.all_gather(up_mine, "fsdp", axis=1, tiled=True)
    partner = [(i, i ^ 1) for i in range(dp_size)]
    down_other = lax.ppermute(down_mine, "dp", partner)
    up_other = lax.ppermute(up_mine, "dp", partner)

    slot_iota = lax.broadcasted_iota(jnp.int32, bag_ids.shape, 2)
    live_ids = jnp.where(slot_iota < bag_counts[:, :, None], bag_ids, vocab_rows)
    send_ids = live_ids.reshape(row_count, table_count * slot_count)
    got_ids = lax.all_to_all(send_ids, "dp", split_axis=1, concat_axis=0, tiled=True)
    sample_count = got_ids.shape[0]
    ids_flat = got_ids.reshape(-1)

    table_f32 = jnp.concatenate(
        [emb_table.astype(jnp.float32), jnp.zeros((ZERO_ROWS, col_piece), jnp.float32)]
    )
    pooled_local = pool_rows(ids_flat, table_f32, slot_count)
    pooled = lax.all_to_all(pooled_local, "dp", split_axis=0, concat_axis=1, tiled=True)

    upstream = cotangent.astype(jnp.float32)
    grad_gate = (upstream * pooled.astype(jnp.float32)).astype(jnp.bfloat16)
    contract = (((1,), (1,)), ((), ()))
    grad_low_mine = lax.dot_general(
        grad_gate, up_mine, contract, preferred_element_type=jnp.float32
    ).astype(jnp.bfloat16)
    grad_low_other = lax.dot_general(
        grad_gate, up_other, contract, preferred_element_type=jnp.float32
    ).astype(jnp.bfloat16)
    down_mine, grad_low_mine, grad_low_other = lax.optimization_barrier(
        (down_mine, grad_low_mine, grad_low_other)
    )
    low_mine = jnp.dot(pooled, down_mine, preferred_element_type=jnp.float32).astype(jnp.bfloat16)
    low_other = jnp.dot(pooled, down_other, preferred_element_type=jnp.float32).astype(jnp.bfloat16)
    low_mine = lax.optimization_barrier(low_mine)
    low_other = lax.optimization_barrier(low_other)
    gate_value = (
        jnp.dot(low_mine, up_mine, preferred_element_type=jnp.float32)
        + jnp.dot(low_other, up_other, preferred_element_type=jnp.float32)
        + cross_bias
    )
    back_term = lax.dot_general(
        grad_low_mine, down_mine, contract, preferred_element_type=jnp.float32
    ) + lax.dot_general(grad_low_other, down_other, contract, preferred_element_type=jnp.float32)
    grad_pooled = (upstream * (gate_value + 1.0) + back_term).astype(jnp.bfloat16)
    grad_local = lax.all_to_all(grad_pooled, "dp", split_axis=1, concat_axis=0, tiled=True)
    partial_value = scatter_rows(
        ids_flat, grad_local, vocab_rows, slot_count
    )
    summed = lax.psum_scatter(
        partial_value, "fsdp", scatter_dimension=0, tiled=True
    )
    return summed.astype(jnp.float32)


def solution(mesh):
    placed = (
        P(("dp", "fsdp"), None, None),
        P(("dp", "fsdp"), None),
        P(None, "dp"),
        P("fsdp", None),
        P(None, "fsdp"),
        P(),
        P(("dp", "fsdp"), None),
    )
    return jax.shard_map(
        on_device, mesh=mesh, in_specs=placed, out_specs=P("fsdp", "dp"), check_vma=False
    )
```
